128 devices in a mesh: dp: 8 (over z, core), ctx: 16 (over y, x).
Axes of the slice: x: 4, y: 4, z: 4, core: 2. Of those that a mesh axis runs over, the one named last changes fastest.
Arguments:
- queries: bfloat16 [8, 2048, 6144], P('dp', 'ctx'), may hold values from -6 to 6
- kv_proj: bfloat16 [8, 4096, 1024], P('dp', 'ctx'), may hold values from -6 to 6
- hidden: bfloat16 [8, 4096, 12288], P('dp', 'ctx'), may hold values from -0.119628906 to 0.119628906
- grad_out: bfloat16 [8, 2048, 6144], P('dp', 'ctx'), may hold values from -6 to 6
- doc_lengths: int32 [8, 256], P('dp'), may hold values from 1 to 8192, 262144 in all within a row
- slab_offsets: int32 [8], P('dp'), may hold values from 0 to 260096
Outputs:
- attended: bfloat16 [8, 2048, 6144], P('dp', 'ctx')
- grad_queries: bfloat16 [8, 2048, 6144], P('dp', 'ctx')
- grad_kv: bfloat16 [8, 4096, 1024], P('dp', 'ctx')
- grad_weight: float32 [12288, 1024], P('ctx', 'dp')
The draws below stay inside these ranges and needn't reach their ends.
All inputs are finite; a program needn't handle non-finite values.
Results may differ from the reference program's by a relative error of at most 0.025.
Values may be sent and summed in bfloat16 or wider, within the bound.
No kernel may reach another device: no remote copies, remote signals or barrier semaphores. Data moves between devices by JAX's collectives and lax.ppermute only.
A program may use at most 192 MiB of HBM per device.

```python
import math
import jax
import jax.numpy as jnp
import numpy as np
from jax import lax

D = 12288
HEAD_FEATURES = 128
QUERY_HEADS = 48
KEY_VALUE_HEADS = 4
WINDOW = 2048
SEQ_LEN = 262144
NDOCS = 256
MOST = 8192
PACKED_SEQUENCES = 8
SLAB = 2048
KEY_POSITIONS = 4096


def paired_draw(key):
    base = jax.random.fold_in(key, 811)
    key_query, key_pair = jax.random.split(base, 2)
    query_shape = (PACKED_SEQUENCES, SLAB, QUERY_HEADS * HEAD_FEATURES)
    key_value_shape = (PACKED_SEQUENCES, KEY_POSITIONS, KEY_VALUE_HEADS * 2 * HEAD_FEATURES)
    query_vals = jnp.clip(jax.random.normal(key_query, query_shape, jnp.float32), -6.0, 6.0)
    key_value_entries = jnp.clip(jax.random.normal(key_pair, key_value_shape, jnp.float32), -6.0, 6.0)
    return (query_vals, key_value_entries)


def draw_queries(key, part):
    return paired_draw(key)[0].astype(jnp.bfloat16)


def draw_kv_proj(key, part):
    return paired_draw(key)[1].astype(jnp.bfloat16)


def place_ends(values, own_key, least, largest):
    longest = values.shape.index(max(values.shape))
    spots = []
    for shift in (0, 1):
        where = [jax.random.randint(jax.random.fold_in(own_key, axis), (), 0, length) for axis, length in enumerate(values.shape)]
        where[longest] = (where[longest] + shift) % values.shape[longest]
        spots.append(tuple(where))
    return values.at[spots[0]].set(least).at[spots[1]].set(largest)


def spiked(entries, own_key, source, target, parts, factor):
    def block_of(position):
        return (jnp.arange(entries.shape[position]) // (entries.shape[position] // parts)).reshape((-1,) + (1,) * (entries.ndim - 1 - position))

    first = jax.random.permutation(own_key, parts)[block_of(target)]
    other_side = (block_of(target) + parts // 2) % parts
    return jnp.where((block_of(source) == first) | (block_of(source) == other_side), factor * entries, entries)


def shard_levels(key, dims, shards, smallest, largest):
    def one(position, parts):
        steps = jax.random.uniform(jax.random.fold_in(jax.random.fold_in(key, 6), position), (parts,), jnp.float32, smallest / len(shards), largest / len(shards))
        return jnp.repeat(jnp.exp(steps), dims[position] // parts).reshape((-1,) + (1,) * (len(dims) - position - 1))

    level = one(*shards[0])
    for cut in shards[1:]:
        level = level * one(*cut)
    return level


def split_up(number_of, total, most, lean):
    portions = [(1 << 20) // math.isqrt(standing ** lean) + 1 for standing in range(2, number_of + 1)]
    surplus, holding = total - most - (number_of - 1), [1] * (number_of - 1)
    while surplus > 0:
        candidates = [i for i in range(number_of - 1) if holding[i] < most]
        mass, left = sum([portions[i] for i in candidates]), surplus
        for i in candidates:
            more = min(most - holding[i], max(1, left * portions[i] // mass), surplus)
            holding[i] = holding[i] + more
            surplus = surplus - more
    return np.array([most] + holding)


def uneven(key, number_of, total, reach, skew):
    if number_of == 2:
        one = jax.random.randint(key, (), max(1, total - reach), min(reach, total - 1) + 1)
        return jnp.stack([one, total - one])
    sizes = jnp.asarray(split_up(number_of, total, reach, skew), jnp.int32)
    couples = (number_of - 1) // 2
    giver, sink = sizes[1:1 + 2 * couples:2], sizes[2:2 + 2 * couples:2]
    slack = jnp.minimum(giver - 1, reach - sink)
    shifted = jax.random.randint(jax.random.fold_in(key, 1), (couples,), 0, 1 << 20) % (slack + 1)
    sizes = sizes.at[1:1 + 2 * couples:2].set(giver - shifted).at[2:2 + 2 * couples:2].set(sink + shifted)
    return sizes[jax.random.permutation(jax.random.fold_in(key, 2), number_of)]


def bell_draw(key, dims, spread, most, pieces=(), kind=jnp.bfloat16):
    drawn = jax.random.normal(key, dims, jnp.float32) * spread
    if len(pieces) > 0:
        drawn = shard_levels(key, dims, pieces, -0.22, 0.18) * drawn
    return jnp.clip(drawn, min=-most, max=most).astype(kind)


def gaussian_with(stream_key, shape, deviation, bound, cuts, heavy, held_as=jnp.bfloat16):
    drawn = deviation * jax.random.normal(stream_key, shape, jnp.float32)
    if cuts:
        drawn = drawn * shard_levels(stream_key, shape, cuts, -0.22, 0.18)
    return jnp.clip(spiked(drawn, jax.random.fold_in(stream_key, 3), *heavy), -bound, bound).astype(held_as)


def setup_inputs(seed: int = 0) -> dict:
    arg_keys = jax.random.split(jax.random.key(seed), 7)
    return {
        "queries": draw_queries(jax.random.fold_in(arg_keys[6], 71), 0),
        "kv_proj": draw_kv_proj(jax.random.fold_in(arg_keys[6], 71), 0),
        "hidden": gaussian_with(arg_keys[2], (PACKED_SEQUENCES, KEY_POSITIONS, D), 0.02, 0.119628906, ((0, 8), (1, 16)), (1, 2, 16, 2.0)),
        "grad_out": bell_draw(arg_keys[3], (PACKED_SEQUENCES, SLAB, QUERY_HEADS * HEAD_FEATURES), 1.0, 6.0, ((0, 8), (1, 16))),
        "doc_lengths": jax.vmap(lambda own: uneven(own, NDOCS, SEQ_LEN, MOST, 2))(jax.random.split(arg_keys[4], PACKED_SEQUENCES)).reshape((PACKED_SEQUENCES, NDOCS)).astype(jnp.int32),
        "slab_offsets": place_ends(jax.random.randint(arg_keys[5], (PACKED_SEQUENCES,), 0, SEQ_LEN - SLAB + 1), jax.random.fold_in(arg_keys[5], 1), 0, SEQ_LEN - SLAB).astype(jnp.int32),
    }


def doc_index(positions, bounds):
    return jnp.sum((bounds[None, :] <= positions[:, None]).astype(jnp.int32), axis=1, dtype=jnp.int32)


def band_mask(anchor, row_count, key_span, offset, bounds):
    query_index = anchor + jnp.arange(row_count, dtype=jnp.int32)
    key_index = anchor + jnp.arange(key_span, dtype=jnp.int32)
    query_pos = offset + query_index
    key_pos = offset - WINDOW + key_index
    same_doc = doc_index(query_pos, bounds)[:, None] == doc_index(key_pos, bounds)[None, :]
    after_query = key_index[None, :] > query_index[:, None]
    within = key_index[None, :] <= query_index[:, None] + WINDOW
    return after_query & within & (key_pos >= 0)[None, :] & same_doc


def band_block(query_block, key_block, value_block, upstream_gradient, allowed):
    factor = HEAD_FEATURES ** -0.5
    f32 = jnp.float32
    scores = jnp.einsum("qhgd,khd->hgqk", query_block.astype(f32), key_block.astype(f32)) * factor
    scores = jnp.where(allowed[None, None], scores, -1e30)
    maxima = jnp.max(scores, axis=-1, keepdims=True)
    raised = jnp.exp(scores - maxima)
    weights = raised / jnp.sum(raised, axis=-1, keepdims=True)
    weights_low = weights.astype(jnp.bfloat16)
    attended = jnp.einsum("hgqk,khd->qhgd", weights_low.astype(f32), value_block.astype(f32)).astype(jnp.bfloat16)
    grad_probs = jnp.einsum("qhgd,khd->hgqk", upstream_gradient.astype(f32), value_block.astype(f32))
    deltas = jnp.einsum("qhgd,qhgd->hgq", upstream_gradient.astype(f32), attended.astype(f32))
    grad_scores = (weights * (grad_probs - deltas[..., None]) * factor).astype(jnp.bfloat16)
    grad_query = jnp.einsum("hgqk,khd->qhgd", grad_scores.astype(f32), key_block.astype(f32)).astype(jnp.bfloat16)
    grad_key = jnp.einsum("hgqk,qhgd->khd", grad_scores.astype(f32), query_block.astype(f32))
    grad_value = jnp.einsum("hgqk,qhgd->khd", weights_low.astype(f32), upstream_gradient.astype(f32))
    return attended, grad_query, jnp.stack([grad_key, grad_value], axis=2)


def band_attention(query_all, upstream_all, pair_all, anchor, offset, bounds, block_rows):
    query_total_count = query_all.shape[0]
    key_total_count = pair_all.shape[0]
    head_count = query_all.shape[1]
    key_span = block_rows + WINDOW

    def step(running, block_index):
        first_row = block_index * block_rows
        query_block = lax.dynamic_slice_in_dim(query_all, first_row, block_rows, 0)
        upstream_gradient = lax.dynamic_slice_in_dim(upstream_all, first_row, block_rows, 0)
        pair_block = lax.dynamic_slice_in_dim(pair_all, first_row, key_span, 0)
        allowed = band_mask(anchor + first_row, block_rows, key_span, offset, bounds)
        attended, grad_query, grad_pair = band_block(query_block, pair_block[:, :, 0], pair_block[:, :, 1], upstream_gradient, allowed)
        previous = lax.dynamic_slice_in_dim(running, first_row, key_span, 0)
        running = lax.dynamic_update_slice_in_dim(running, previous + grad_pair, first_row, 0)
        return running, (attended, grad_query)

    initial = jnp.zeros((key_total_count, head_count, 2, HEAD_FEATURES), jnp.float32)
    grads, outputs = lax.scan(step, initial, jnp.arange(query_total_count // block_rows, dtype=jnp.int32))
    attended, grad_query = outputs
    return attended.reshape(query_total_count, -1), grad_query.reshape(query_total_count, -1), grads.reshape(key_total_count, -1)


def reference(queries, kv_proj, hidden, grad_out, doc_lengths, slab_offsets):
    queries_per_group = QUERY_HEADS // KEY_VALUE_HEADS

    def one_sequence(running, inputs):
        query_matrix_rows, key_matrix_rows, hidden_rows, upstream_gradient, lengths, offset = inputs
        bounds = jnp.cumsum(lengths, dtype=jnp.int32)
        query_total_count = query_matrix_rows.shape[0]
        attended, grad_query, grad_keys = band_attention(
            query_matrix_rows.reshape(query_total_count, KEY_VALUE_HEADS, queries_per_group, HEAD_FEATURES),
            upstream_gradient.reshape(query_total_count, KEY_VALUE_HEADS, queries_per_group, HEAD_FEATURES),
            key_matrix_rows.reshape(key_matrix_rows.shape[0], KEY_VALUE_HEADS, 2, HEAD_FEATURES),
            0, offset, bounds, min(512, query_total_count))
        grad_low = grad_keys.astype(jnp.bfloat16)
        running = running + jnp.dot(hidden_rows.T, grad_low, preferred_element_type=jnp.float32)
        return running, (attended, grad_query, grad_low)

    initial = jnp.zeros((hidden.shape[2], kv_proj.shape[2]), jnp.float32)
    grad_weight, outputs = lax.scan(one_sequence, initial, (queries, kv_proj, hidden, grad_out, doc_lengths, slab_offsets))
    attended, grad_queries, grad_kv = outputs
    return (attended, grad_queries, grad_kv, grad_weight)
```

```python
import functools

import jax
import jax.numpy as jnp
from jax import lax
from jax.experimental import pallas as pl
from jax.experimental.pallas import tpu as pltpu
from jax.sharding import PartitionSpec as P

HEAD_FEATURES = 128
KEY_VALUE_HEADS = 4
WINDOW = 2048
BLOCK_QUERIES = 256


def doc_index(positions, bounds):
    return jnp.sum(
        (bounds[None, :] <= positions[:, None]).astype(jnp.int32), axis=1, dtype=jnp.int32
    )


def attention_kernel(qdoc_ref, kdoc_ref, q_ref, go_ref, kv_ref, att_ref, dq_ref, dkv_ref, *, bq, span):
    qb = pl.program_id(0)
    h = pl.program_id(1)
    f32 = jnp.float32
    bf16 = jnp.bfloat16
    factor = HEAD_FEATURES ** (-0.5)

    @pl.when((qb == 0) & (h == 0))
    def _():
        dkv_ref[...] = jnp.zeros_like(dkv_ref)

    start = pl.multiple_of(qb * bq, bq)
    k = kv_ref[pl.ds(start, span), 0:HEAD_FEATURES]
    v = kv_ref[pl.ds(start, span), HEAD_FEATURES : 2 * HEAD_FEATURES]
    q = q_ref[...]
    go = go_ref[...]
    nt = (((1,), (1,)), ((), ()))
    tn = (((0,), (0,)), ((), ()))
    scores = lax.dot_general(q, k, nt, preferred_element_type=f32) * factor
    row = lax.broadcasted_iota(jnp.int32, (bq, span), 0)
    col = lax.broadcasted_iota(jnp.int32, (bq, span), 1)
    same_doc = qdoc_ref[...] == kdoc_ref[:, pl.ds(start, span)]
    allowed = (col > row) & (col <= row + WINDOW) & same_doc
    scores = jnp.where(allowed, scores, -1e30)
    maxima = jnp.max(scores, axis=1, keepdims=True)
    raised = jnp.exp(scores - maxima)
    weights = raised / jnp.sum(raised, axis=1, keepdims=True)
    weights_low = weights.astype(bf16)
    att = jnp.dot(weights_low, v, preferred_element_type=f32).astype(bf16)
    att_ref[...] = att
    grad_probs = lax.dot_general(go, v, nt, preferred_element_type=f32)
    deltas = jnp.sum(go.astype(f32) * att.astype(f32), axis=1, keepdims=True)
    grad_scores = (weights * (grad_probs - deltas) * factor).astype(bf16)
    dq_ref[...] = jnp.dot(grad_scores, k, preferred_element_type=f32).astype(bf16)
    dk = lax.dot_general(grad_scores, q, tn, preferred_element_type=f32)
    dv = lax.dot_general(weights_low, go, tn, preferred_element_type=f32)
    dkv_ref[pl.ds(start, span), 0:HEAD_FEATURES] += dk
    dkv_ref[pl.ds(start, span), HEAD_FEATURES : 2 * HEAD_FEATURES] += dv


def head_attention(head_queries, head_upstream, head_keys, q_doc, k_doc):
    rows = head_queries.shape[0]
    keys = head_keys.shape[0]
    heads_here = head_queries.shape[1] // HEAD_FEATURES
    bq = min(BLOCK_QUERIES, rows)
    span = bq + WINDOW
    grid = (rows // bq, heads_here)
    kernel = functools.partial(attention_kernel, bq=bq, span=span)
    flops = 12 * heads_here * rows * span * HEAD_FEATURES
    bytes_accessed = 2 * (4 * rows * heads_here * HEAD_FEATURES + keys * 2 * HEAD_FEATURES) + 4 * keys * 2 * HEAD_FEATURES
    return pl.pallas_call(
        kernel,
        grid=grid,
        in_specs=[
            pl.BlockSpec((bq, 1), lambda i, h: (i, 0)),
            pl.BlockSpec((1, keys), lambda i, h: (0, 0)),
            pl.BlockSpec((bq, HEAD_FEATURES), lambda i, h: (i, h)),
            pl.BlockSpec((bq, HEAD_FEATURES), lambda i, h: (i, h)),
            pl.BlockSpec((keys, 2 * HEAD_FEATURES), lambda i, h: (0, 0)),
        ],
        out_specs=[
            pl.BlockSpec((bq, HEAD_FEATURES), lambda i, h: (i, h)),
            pl.BlockSpec((bq, HEAD_FEATURES), lambda i, h: (i, h)),
            pl.BlockSpec((keys, 2 * HEAD_FEATURES), lambda i, h: (0, 0)),
        ],
        out_shape=[
            jax.ShapeDtypeStruct(head_queries.shape, jnp.bfloat16),
            jax.ShapeDtypeStruct(head_queries.shape, jnp.bfloat16),
            jax.ShapeDtypeStruct((keys, 2 * HEAD_FEATURES), jnp.float32),
        ],
        compiler_params=pltpu.CompilerParams(
            dimension_semantics=("arbitrary", "arbitrary"), vmem_limit_bytes=60 * 1024 * 1024
        ),
        cost_estimate=pl.CostEstimate(
            flops=flops, transcendentals=heads_here * rows * span, bytes_accessed=bytes_accessed
        ),
        name="band_attention",
    )(q_doc.reshape(rows, 1), k_doc.reshape(1, keys), head_queries, head_upstream, head_keys)


def local(queries, kv_proj, hidden, grad_out, doc_lengths, slab_offsets):
    query_matrix_rows = queries[0]
    upstream_gradient = grad_out[0]
    key_matrix_rows = kv_proj[0]
    hidden_rows = hidden[0]
    bounds = jnp.cumsum(doc_lengths[0], dtype=jnp.int32)
    offset = slab_offsets[0]
    key_value_width = 2 * KEY_VALUE_HEADS * HEAD_FEATURES
    hidden_cols = lax.all_to_all(hidden_rows, "ctx", split_axis=1, concat_axis=0, tiled=True)
    repeat_heads = lax.axis_size("ctx") // KEY_VALUE_HEADS
    key_total_count = key_matrix_rows.shape[0]
    copies = jnp.broadcast_to(
        key_matrix_rows.reshape(key_total_count, KEY_VALUE_HEADS, 1, 2 * HEAD_FEATURES),
        (key_total_count, KEY_VALUE_HEADS, repeat_heads, 2 * HEAD_FEATURES),
    ).reshape(key_total_count, KEY_VALUE_HEADS * repeat_heads * 2 * HEAD_FEATURES)
    head_queries, head_upstream, head_keys = (
        lax.all_to_all(query_matrix_rows, "ctx", split_axis=1, concat_axis=0, tiled=True),
        lax.all_to_all(upstream_gradient, "ctx", split_axis=1, concat_axis=0, tiled=True),
        lax.all_to_all(copies, "ctx", split_axis=1, concat_axis=0, tiled=True),
    )
    rows = head_queries.shape[0]
    keys = head_keys.shape[0]
    query_pos = offset + jnp.arange(rows, dtype=jnp.int32)
    key_pos = offset - WINDOW + jnp.arange(keys, dtype=jnp.int32)
    q_doc = doc_index(query_pos, bounds)
    k_doc = jnp.where(key_pos >= 0, doc_index(key_pos, bounds), -1)
    attended_heads, grad_query_heads, grad_head = head_attention(
        head_queries, head_upstream, head_keys, q_doc, k_doc
    )
    attended, grad_query = (
        lax.all_to_all(attended_heads, "ctx", split_axis=0, concat_axis=1, tiled=True),
        lax.all_to_all(grad_query_heads, "ctx", split_axis=0, concat_axis=1, tiled=True),
    )
    partial_sums = lax.all_to_all(
        grad_head.astype(jnp.bfloat16), "ctx", split_axis=0, concat_axis=1, tiled=True
    )
    grad_keys = jnp.sum(
        partial_sums.reshape(
            partial_sums.shape[0], KEY_VALUE_HEADS, repeat_heads, 2 * HEAD_FEATURES
        ).astype(jnp.float32),
        axis=2,
    ).reshape(partial_sums.shape[0], key_value_width)
    grad_low = grad_keys.astype(jnp.bfloat16)
    local_weight = jnp.einsum(
        "kd,kc->dc",
        hidden_cols,
        lax.all_gather(grad_low, "ctx", axis=0, tiled=True),
        preferred_element_type=jnp.float32,
    )
    grad_weight = lax.psum_scatter(
        local_weight.astype(jnp.bfloat16), "dp", scatter_dimension=1, tiled=True
    ).astype(jnp.float32)
    return (attended[None], grad_query[None], grad_low[None], grad_weight)


def solution(mesh):
    in_specs = (
        P("dp", "ctx", None),
        P("dp", "ctx", None),
        P("dp", "ctx", None),
        P("dp", "ctx", None),
        P("dp", None),
        P("dp"),
    )
    out_specs = (P("dp", "ctx", None), P("dp", "ctx", None), P("dp", "ctx", None), P("ctx", "dp"))
    return jax.shard_map(local, mesh=mesh, in_specs=in_specs, out_specs=out_specs, check_vma=False)
```

```python
import functools

import jax
import jax.numpy as jnp
from jax import lax
from jax.experimental import pallas as pl
from jax.experimental.pallas import tpu as pltpu
from jax.sharding import PartitionSpec as P


HEAD_FEATURES = 128
KEY_VALUE_HEADS = 4
WINDOW = 2048
BLOCK_QUERIES = 256


def doc_index(positions, bounds):
    return jnp.sum(
        (bounds[None, :] <= positions[:, None]).astype(jnp.int32), axis=1, dtype=jnp.int32
    )


def attention_kernel(qdoc_ref, kdoc_ref, q_ref, go_ref, kv_ref, att_ref, dq_ref, dkv_ref, *, bq, span):
    qb = pl.program_id(0)
    h = pl.program_id(1)
    f32 = jnp.float32
    bf16 = jnp.bfloat16
    factor = HEAD_FEATURES ** (-0.5)

    @pl.when((qb == 0) & (h == 0))
    def _():
        dkv_ref[...] = jnp.zeros_like(dkv_ref)

    start = pl.multiple_of(qb * bq, bq)
    k = kv_ref[pl.ds(start, span), 0:HEAD_FEATURES]
    v = kv_ref[pl.ds(start, span), HEAD_FEATURES : 2 * HEAD_FEATURES]
    q = q_ref[...]
    go = go_ref[...]
    nt = (((1,), (1,)), ((), ()))
    tn = (((0,), (0,)), ((), ()))
    scores = lax.dot_general(q, k, nt, preferred_element_type=f32) * factor
    row = lax.broadcasted_iota(jnp.int32, (bq, span), 0)
    col = lax.broadcasted_iota(jnp.int32, (bq, span), 1)
    same_doc = qdoc_ref[...] == kdoc_ref[:, pl.ds(start, span)]
    allowed = (col > row) & (col <= row + WINDOW) & same_doc
    scores = jnp.where(allowed, scores, -1e30)
    maxima = jnp.max(scores, axis=1, keepdims=True)
    raised = jnp.exp(scores - maxima)
    weights = raised / jnp.sum(raised, axis=1, keepdims=True)
    weights_low = weights.astype(bf16)
    att = jnp.dot(weights_low, v, preferred_element_type=f32).astype(bf16)
    att_ref[...] = att
    grad_probs = lax.dot_general(go, v, nt, preferred_element_type=f32)
    deltas = jnp.sum(go.astype(f32) * att.astype(f32), axis=1, keepdims=True)
    grad_scores = (weights * (grad_probs - deltas) * factor).astype(bf16)
    dq_ref[...] = jnp.dot(grad_scores, k, preferred_element_type=f32).astype(bf16)
    dk = lax.dot_general(grad_scores, q, tn, preferred_element_type=f32)
    dv = lax.dot_general(weights_low, go, tn, preferred_element_type=f32)
    dkv_ref[pl.ds(start, span), 0:HEAD_FEATURES] += dk
    dkv_ref[pl.ds(start, span), HEAD_FEATURES : 2 * HEAD_FEATURES] += dv


def head_attention(head_queries, head_upstream, head_keys, q_doc, k_doc):
    rows = head_queries.shape[0]
    keys = head_keys.shape[0]
    heads_here = head_queries.shape[1] // HEAD_FEATURES
    bq = min(BLOCK_QUERIES, rows)
    span = bq + WINDOW
    grid = (rows // bq, heads_here)
    kernel = functools.partial(attention_kernel, bq=bq, span=span)
    flops = 12 * heads_here * rows * span * HEAD_FEATURES
    bytes_accessed = 2 * (4 * rows * heads_here * HEAD_FEATURES + keys * 2 * HEAD_FEATURES) + 4 * keys * 2 * HEAD_FEATURES
    return pl.pallas_call(
        kernel,
        grid=grid,
        in_specs=[
            pl.BlockSpec((bq, 1), lambda i, h: (i, 0)),
            pl.BlockSpec((1, keys), lambda i, h: (0, 0)),
            pl.BlockSpec((bq, HEAD_FEATURES), lambda i, h: (i, h)),
            pl.BlockSpec((bq, HEAD_FEATURES), lambda i, h: (i, h)),
            pl.BlockSpec((keys, 2 * HEAD_FEATURES), lambda i, h: (0, 0)),
        ],
        out_specs=[
            pl.BlockSpec((bq, HEAD_FEATURES), lambda i, h: (i, h)),
            pl.BlockSpec((bq, HEAD_FEATURES), lambda i, h: (i, h)),
            pl.BlockSpec((keys, 2 * HEAD_FEATURES), lambda i, h: (0, 0)),
        ],
        out_shape=[
            jax.ShapeDtypeStruct(head_queries.shape, jnp.bfloat16),
            jax.ShapeDtypeStruct(head_queries.shape, jnp.bfloat16),
            jax.ShapeDtypeStruct((keys, 2 * HEAD_FEATURES), jnp.float32),
        ],
        compiler_params=pltpu.CompilerParams(
            dimension_semantics=("arbitrary", "arbitrary"), vmem_limit_bytes=60 * 1024 * 1024
        ),
        cost_estimate=pl.CostEstimate(
            flops=flops, transcendentals=heads_here * rows * span, bytes_accessed=bytes_accessed
        ),
        name="band_attention",
    )(q_doc.reshape(rows, 1), k_doc.reshape(1, keys), head_queries, head_upstream, head_keys)


def weight_gradient(hidden_rows, grad_low):
    dp = lax.axis_size("dp")
    ctx = lax.axis_size("ctx")
    rows, features = hidden_rows.shape
    piece = features // (ctx * dp)
    width = features // dp
    me = lax.axis_index("dp")
    interleaved = hidden_rows.reshape(rows, ctx, dp, piece).transpose(2, 0, 1, 3).reshape(dp, rows, width)
    received = [lax.dynamic_index_in_dim(interleaved, me, 0, keepdims=False)]
    for shift in range(1, dp):
        outgoing = lax.dynamic_index_in_dim(interleaved, (me + shift) % dp, 0, keepdims=False)
        pairs = [(i, (i + shift) % dp) for i in range(dp)]
        received.append(lax.ppermute(outgoing, "dp", pairs))
    hidden_dp = jnp.concatenate(received, axis=0)
    grad_all = lax.all_gather(grad_low, "dp", axis=0, tiled=False)
    grad_dp = jnp.concatenate(
        [lax.dynamic_index_in_dim(grad_all, (me - shift) % dp, 0, keepdims=False) for shift in range(dp)],
        axis=0,
    )
    partial = jnp.einsum("kd,kc->dc", hidden_dp, grad_dp, preferred_element_type=jnp.float32)
    reduced = lax.psum_scatter(partial, "ctx", scatter_dimension=0, tiled=True)
    return lax.all_to_all(reduced, "dp", split_axis=1, concat_axis=0, tiled=True)


def local_body(queries, kv_proj, hidden, grad_out, doc_lengths, slab_offsets):
    query_matrix_rows = queries[0]
    upstream_gradient = grad_out[0]
    key_matrix_rows = kv_proj[0]
    hidden_rows = hidden[0]
    bounds = jnp.cumsum(doc_lengths[0], dtype=jnp.int32)
    offset = slab_offsets[0]
    key_value_width = 2 * KEY_VALUE_HEADS * HEAD_FEATURES
    repeat_heads = lax.axis_size("ctx") // KEY_VALUE_HEADS
    key_total_count = key_matrix_rows.shape[0]
    copies = jnp.broadcast_to(
        key_matrix_rows.reshape(key_total_count, KEY_VALUE_HEADS, 1, 2 * HEAD_FEATURES),
        (key_total_count, KEY_VALUE_HEADS, repeat_heads, 2 * HEAD_FEATURES),
    ).reshape(key_total_count, KEY_VALUE_HEADS * repeat_heads * 2 * HEAD_FEATURES)
    head_queries, head_upstream, head_keys = (
        lax.all_to_all(query_matrix_rows, "ctx", split_axis=1, concat_axis=0, tiled=True),
        lax.all_to_all(upstream_gradient, "ctx", split_axis=1, concat_axis=0, tiled=True),
        lax.all_to_all(copies, "ctx", split_axis=1, concat_axis=0, tiled=True),
    )
    rows = head_queries.shape[0]
    keys = head_keys.shape[0]
    query_pos = offset + jnp.arange(rows, dtype=jnp.int32)
    key_pos = offset - WINDOW + jnp.arange(keys, dtype=jnp.int32)
    q_doc = doc_index(query_pos, bounds)
    k_doc = jnp.where(key_pos >= 0, doc_index(key_pos, bounds), -1)
    attended_heads, grad_query_heads, grad_head = head_attention(head_queries, head_upstream, head_keys, q_doc, k_doc)
    attended, grad_query = (
        lax.all_to_all(attended_heads, "ctx", split_axis=0, concat_axis=1, tiled=True),
        lax.all_to_all(grad_query_heads, "ctx", split_axis=0, concat_axis=1, tiled=True),
    )
    partial_sums = lax.all_to_all(
        grad_head.astype(jnp.bfloat16), "ctx", split_axis=0, concat_axis=1, tiled=True
    )
    grad_keys = jnp.sum(
        partial_sums.reshape(
            partial_sums.shape[0], KEY_VALUE_HEADS, repeat_heads, 2 * HEAD_FEATURES
        ).astype(jnp.float32),
        axis=2,
    ).reshape(partial_sums.shape[0], key_value_width)
    grad_low = grad_keys.astype(jnp.bfloat16)
    grad_weight = weight_gradient(hidden_rows, grad_low)
    return (attended[None], grad_query[None], grad_low[None], grad_weight)


def solution(mesh):
    in_specs = (
        P("dp", "ctx", None),
        P("dp", "ctx", None),
        P("dp", "ctx", None),
        P("dp", "ctx", None),
        P("dp", None),
        P("dp"),
    )
    out_specs = (P("dp", "ctx", None), P("dp", "ctx", None), P("dp", "ctx", None), P("ctx", "dp"))
    return jax.shard_map(local_body, mesh=mesh, in_specs=in_specs, out_specs=out_specs, check_vma=False)
```

```python
import functools

import jax
import jax.numpy as jnp
from jax import lax
from jax.experimental import pallas as pl
from jax.experimental.pallas import tpu as pltpu
from jax.sharding import PartitionSpec as P


HEAD_FEATURES = 128
KEY_VALUE_HEADS = 4
WINDOW = 2048
BLOCK_QUERIES = 256


def doc_index(positions, bounds):
    return jnp.sum(
        (bounds[None, :] <= positions[:, None]).astype(jnp.int32), axis=1, dtype=jnp.int32
    )


def attention_kernel(qdoc_ref, kdoc_ref, q_ref, go_ref, kv_ref, att_ref, dq_ref, dkv_ref, *, bq, span):
    qb = pl.program_id(0)
    h = pl.program_id(1)
    f32 = jnp.float32
    bf16 = jnp.bfloat16
    factor = HEAD_FEATURES ** (-0.5)

    @pl.when((qb == 0) & (h == 0))
    def _():
        dkv_ref[...] = jnp.zeros_like(dkv_ref)

    start = pl.multiple_of(qb * bq, bq)
    k = kv_ref[pl.ds(start, span), 0:HEAD_FEATURES]
    v = kv_ref[pl.ds(start, span), HEAD_FEATURES : 2 * HEAD_FEATURES]
    q = q_ref[...]
    go = go_ref[...]
    nt = (((1,), (1,)), ((), ()))
    tn = (((0,), (0,)), ((), ()))
    scores = lax.dot_general(q, k, nt, preferred_element_type=f32) * factor
    row = lax.broadcasted_iota(jnp.int32, (bq, span), 0)
    col = lax.broadcasted_iota(jnp.int32, (bq, span), 1)
    same_doc = qdoc_ref[...] == kdoc_ref[:, pl.ds(start, span)]
    allowed = (col > row) & (col <= row + WINDOW) & same_doc
    scores = jnp.where(allowed, scores, -1e30)
    maxima = jnp.max(scores, axis=1, keepdims=True)
    raised = jnp.exp(scores - maxima)
    weights = raised / jnp.sum(raised, axis=1, keepdims=True)
    weights_low = weights.astype(bf16)
    att = jnp.dot(weights_low, v, preferred_element_type=f32).astype(bf16)
    att_ref[...] = att
    grad_probs = lax.dot_general(go, v, nt, preferred_element_type=f32)
    deltas = jnp.sum(go.astype(f32) * att.astype(f32), axis=1, keepdims=True)
    grad_scores = (weights * (grad_probs - deltas) * factor).astype(bf16)
    dq_ref[...] = jnp.dot(grad_scores, k, preferred_element_type=f32).astype(bf16)
    dk = lax.dot_general(grad_scores, q, tn, preferred_element_type=f32)
    dv = lax.dot_general(weights_low, go, tn, preferred_element_type=f32)
    dkv_ref[pl.ds(start, span), 0:HEAD_FEATURES] += dk
    dkv_ref[pl.ds(start, span), HEAD_FEATURES : 2 * HEAD_FEATURES] += dv


def head_attention(head_queries, head_upstream, head_keys, q_doc, k_doc):
    rows = head_queries.shape[0]
    keys = head_keys.shape[0]
    heads_here = head_queries.shape[1] // HEAD_FEATURES
    bq = min(BLOCK_QUERIES, rows)
    span = bq + WINDOW
    grid = (rows // bq, heads_here)
    kernel = functools.partial(attention_kernel, bq=bq, span=span)
    flops = 12 * heads_here * rows * span * HEAD_FEATURES
    bytes_accessed = 2 * (4 * rows * heads_here * HEAD_FEATURES + keys * 2 * HEAD_FEATURES) + 4 * keys * 2 * HEAD_FEATURES
    return pl.pallas_call(
        kernel,
        grid=grid,
        in_specs=[
            pl.BlockSpec((bq, 1), lambda i, h: (i, 0)),
            pl.BlockSpec((1, keys), lambda i, h: (0, 0)),
            pl.BlockSpec((bq, HEAD_FEATURES), lambda i, h: (i, h)),
            pl.BlockSpec((bq, HEAD_FEATURES), lambda i, h: (i, h)),
            pl.BlockSpec((keys, 2 * HEAD_FEATURES), lambda i, h: (0, 0)),
        ],
        out_specs=[
            pl.BlockSpec((bq, HEAD_FEATURES), lambda i, h: (i, h)),
            pl.BlockSpec((bq, HEAD_FEATURES), lambda i, h: (i, h)),
            pl.BlockSpec((keys, 2 * HEAD_FEATURES), lambda i, h: (0, 0)),
        ],
        out_shape=[
            jax.ShapeDtypeStruct(head_queries.shape, jnp.bfloat16),
            jax.ShapeDtypeStruct(head_queries.shape, jnp.bfloat16),
            jax.ShapeDtypeStruct((keys, 2 * HEAD_FEATURES), jnp.float32),
        ],
        compiler_params=pltpu.CompilerParams(
            dimension_semantics=("arbitrary", "arbitrary"), vmem_limit_bytes=60 * 1024 * 1024
        ),
        cost_estimate=pl.CostEstimate(
            flops=flops, transcendentals=heads_here * rows * span, bytes_accessed=bytes_accessed
        ),
        name="band_attention",
    )(q_doc.reshape(rows, 1), k_doc.reshape(1, keys), head_queries, head_upstream, head_keys)


def weight_kernel(me_ref, *refs, parts):
    pieces, grad_ref, out_ref = refs[:parts], refs[parts], refs[parts + 1]
    me = me_ref[0]
    total = None
    for shift in range(parts):
        source = lax.rem(me - shift + parts, parts)
        term = lax.dot_general(
            pieces[shift][...], grad_ref[source], (((0,), (0,)), ((), ())),
            preferred_element_type=jnp.float32,
        )
        total = term if total is None else total + term
    out_ref[...] = total.astype(out_ref.dtype)


def stacked_weight_product(me, pieces, grad_all):
    parts = len(pieces)
    rows, width = pieces[0].shape
    columns = grad_all.shape[2]
    tile = 512 if width % 512 == 0 else width
    grid_spec = pltpu.PrefetchScalarGridSpec(
        num_scalar_prefetch=1,
        grid=(width // tile,),
        in_specs=[pl.BlockSpec((rows, tile), lambda i, me: (0, i)) for _ in range(parts)]
        + [pl.BlockSpec((parts, rows, columns), lambda i, me: (0, 0, 0))],
        out_specs=pl.BlockSpec((tile, columns), lambda i, me: (i, 0)),
    )
    return pl.pallas_call(
        functools.partial(weight_kernel, parts=parts),
        grid_spec=grid_spec,
        out_shape=jax.ShapeDtypeStruct((width, columns), jnp.bfloat16),
        compiler_params=pltpu.CompilerParams(
            dimension_semantics=("arbitrary",), vmem_limit_bytes=48 * 1024 * 1024
        ),
        cost_estimate=pl.CostEstimate(
            flops=2 * parts * rows * width * columns,
            transcendentals=0,
            bytes_accessed=2 * parts * rows * (width + columns) + 2 * width * columns,
        ),
        name="weight_product",
    )(jnp.reshape(me, (1,)).astype(jnp.int32), *pieces, grad_all)


def weight_gradient(hidden_rows, grad_low):
    dp = lax.axis_size("dp")
    ctx = lax.axis_size("ctx")
    rows, features = hidden_rows.shape
    piece = features // (ctx * dp)
    width = features // dp
    me = lax.axis_index("dp")
    interleaved = hidden_rows.reshape(rows, ctx, dp, piece).transpose(2, 0, 1, 3).reshape(dp, rows, width)
    received = [lax.dynamic_index_in_dim(interleaved, me, 0, keepdims=False)]
    for shift in range(1, dp):
        outgoing = lax.dynamic_index_in_dim(interleaved, (me + shift) % dp, 0, keepdims=False)
        pairs = [(i, (i + shift) % dp) for i in range(dp)]
        received.append(lax.ppermute(outgoing, "dp", pairs))
    grad_all = lax.all_gather(grad_low, "dp", axis=0, tiled=False)
    partial = stacked_weight_product(me, received, grad_all)
    reduced = lax.psum_scatter(partial, "ctx", scatter_dimension=0, tiled=True)
    return lax.all_to_all(reduced.astype(jnp.float32), "dp", split_axis=1, concat_axis=0, tiled=True)


def local_body(queries, kv_proj, hidden, grad_out, doc_lengths, slab_offsets):
    query_matrix_rows = queries[0]
    upstream_gradient = grad_out[0]
    key_matrix_rows = kv_proj[0]
    hidden_rows = hidden[0]
    bounds = jnp.cumsum(doc_lengths[0], dtype=jnp.int32)
    offset = slab_offsets[0]
    key_value_width = 2 * KEY_VALUE_HEADS * HEAD_FEATURES
    repeat_heads = lax.axis_size("ctx") // KEY_VALUE_HEADS
    key_total_count = key_matrix_rows.shape[0]
    copies = jnp.broadcast_to(
        key_matrix_rows.reshape(key_total_count, KEY_VALUE_HEADS, 1, 2 * HEAD_FEATURES),
        (key_total_count, KEY_VALUE_HEADS, repeat_heads, 2 * HEAD_FEATURES),
    ).reshape(key_total_count, KEY_VALUE_HEADS * repeat_heads * 2 * HEAD_FEATURES)
    head_queries, head_upstream, head_keys = (
        lax.all_to_all(query_matrix_rows, "ctx", split_axis=1, concat_axis=0, tiled=True),
        lax.all_to_all(upstream_gradient, "ctx", split_axis=1, concat_axis=0, tiled=True),
        lax.all_to_all(copies, "ctx", split_axis=1, concat_axis=0, tiled=True),
    )
    rows = head_queries.shape[0]
    keys = head_keys.shape[0]
    query_pos = offset + jnp.arange(rows, dtype=jnp.int32)
    key_pos = offset - WINDOW + jnp.arange(keys, dtype=jnp.int32)
    q_doc = doc_index(query_pos, bounds)
    k_doc = jnp.where(key_pos >= 0, doc_index(key_pos, bounds), -1)
    attended_heads, grad_query_heads, grad_head = head_attention(
        head_queries, head_upstream, head_keys, q_doc, k_doc
    )
    attended, grad_query = (
        lax.all_to_all(attended_heads, "ctx", split_axis=0, concat_axis=1, tiled=True),
        lax.all_to_all(grad_query_heads, "ctx", split_axis=0, concat_axis=1, tiled=True),
    )
    partial_sums = lax.all_to_all(
        grad_head.astype(jnp.bfloat16), "ctx", split_axis=0, concat_axis=1, tiled=True
    )
    grad_keys = jnp.sum(
        partial_sums.reshape(
            partial_sums.shape[0], KEY_VALUE_HEADS, repeat_heads, 2 * HEAD_FEATURES
        ).astype(jnp.float32),
        axis=2,
    ).reshape(partial_sums.shape[0], key_value_width)
    grad_low = grad_keys.astype(jnp.bfloat16)
    grad_weight = weight_gradient(hidden_rows, grad_low)
    return (attended[None], grad_query[None], grad_low[None], grad_weight)


def solution(mesh):
    in_specs = (
        P("dp", "ctx", None),
        P("dp", "ctx", None),
        P("dp", "ctx", None),
        P("dp", "ctx", None),
        P("dp", None),
        P("dp"),
    )
    out_specs = (P("dp", "ctx", None), P("dp", "ctx", None), P("dp", "ctx", None), P("ctx", "dp"))
    return jax.shard_map(local_body, mesh=mesh, in_specs=in_specs, out_specs=out_specs, check_vma=False)
```

```python
import functools

import jax
import jax.numpy as jnp
from jax import lax
from jax.experimental import pallas as pl
from jax.experimental.pallas import tpu as pltpu
from jax.sharding import PartitionSpec as P


HEAD_FEATURES = 128
KEY_VALUE_HEADS = 4
WINDOW = 2048
BLOCK_QUERIES = 256


def doc_index(positions, bounds):
    return jnp.sum(
        (bounds[None, :] <= positions[:, None]).astype(jnp.int32), axis=1, dtype=jnp.int32
    )


def attention_kernel(qdoc_ref, kdoc_ref, q_ref, go_ref, kv_ref, att_ref, dq_ref, dkv_ref, *, bq, span):
    qb = pl.program_id(0)
    h = pl.program_id(1)
    f32 = jnp.float32
    bf16 = jnp.bfloat16
    factor = HEAD_FEATURES ** (-0.5)

    @pl.when((qb == 0) & (h == 0))
    def _():
        dkv_ref[...] = jnp.zeros_like(dkv_ref)

    start = pl.multiple_of(qb * bq, bq)
    k = kv_ref[pl.ds(start, span), 0:HEAD_FEATURES]
    v = kv_ref[pl.ds(start, span), HEAD_FEATURES : 2 * HEAD_FEATURES]
    q = q_ref[...]
    go = go_ref[...]
    nt = (((1,), (1,)), ((), ()))
    tn = (((0,), (0,)), ((), ()))
    scores = lax.dot_general(q, k, nt, preferred_element_type=f32) * factor
    row = lax.broadcasted_iota(jnp.int32, (bq, span), 0)
    col = lax.broadcasted_iota(jnp.int32, (bq, span), 1)
    same_doc = qdoc_ref[...] == kdoc_ref[:, pl.ds(start, span)]
    allowed = (col > row) & (col <= row + WINDOW) & same_doc
    scores = jnp.where(allowed, scores, -1e30)
    maxima = jnp.max(scores, axis=1, keepdims=True)
    raised = jnp.exp(scores - maxima)
    weights = raised * (1.0 / jnp.sum(raised, axis=1, keepdims=True))
    weights_low = weights.astype(bf16)
    att = jnp.dot(weights_low, v, preferred_element_type=f32).astype(bf16)
    att_ref[...] = att
    grad_probs = lax.dot_general(go, v, nt, preferred_element_type=f32)
    deltas = jnp.sum(go.astype(f32) * att.astype(f32), axis=1, keepdims=True)
    grad_scores = (weights * (grad_probs - deltas) * factor).astype(bf16)
    dq_ref[...] = jnp.dot(grad_scores, k, preferred_element_type=f32).astype(bf16)
    dk = lax.dot_general(grad_scores, q, tn, preferred_element_type=f32)
    dv = lax.dot_general(weights_low, go, tn, preferred_element_type=f32)
    dkv_ref[pl.ds(start, span), 0:HEAD_FEATURES] += dk
    dkv_ref[pl.ds(start, span), HEAD_FEATURES : 2 * HEAD_FEATURES] += dv


def head_attention(head_queries, head_upstream, head_keys, q_doc, k_doc):
    rows = head_queries.shape[0]
    keys = head_keys.shape[0]
    heads_here = head_queries.shape[1] // HEAD_FEATURES
    bq = min(BLOCK_QUERIES, rows)
    span = bq + WINDOW
    grid = (rows // bq, heads_here)
    kernel = functools.partial(attention_kernel, bq=bq, span=span)
    flops = 12 * heads_here * rows * span * HEAD_FEATURES
    bytes_accessed = 2 * (4 * rows * heads_here * HEAD_FEATURES + keys * 2 * HEAD_FEATURES) + 4 * keys * 2 * HEAD_FEATURES
    return pl.pallas_call(
        kernel,
        grid=grid,
        in_specs=[
            pl.BlockSpec((bq, 1), lambda i, h: (i, 0)),
            pl.BlockSpec((1, keys), lambda i, h: (0, 0)),
            pl.BlockSpec((bq, HEAD_FEATURES), lambda i, h: (i, h)),
            pl.BlockSpec((bq, HEAD_FEATURES), lambda i, h: (i, h)),
            pl.BlockSpec((keys, 2 * HEAD_FEATURES), lambda i, h: (0, 0)),
        ],
        out_specs=[
            pl.BlockSpec((bq, HEAD_FEATURES), lambda i, h: (i, h)),
            pl.BlockSpec((bq, HEAD_FEATURES), lambda i, h: (i, h)),
            pl.BlockSpec((keys, 2 * HEAD_FEATURES), lambda i, h: (0, 0)),
        ],
        out_shape=[
            jax.ShapeDtypeStruct(head_queries.shape, jnp.bfloat16),
            jax.ShapeDtypeStruct(head_queries.shape, jnp.bfloat16),
            jax.ShapeDtypeStruct((keys, 2 * HEAD_FEATURES), jnp.float32),
        ],
        compiler_params=pltpu.CompilerParams(
            dimension_semantics=("arbitrary", "arbitrary"), vmem_limit_bytes=60 * 1024 * 1024
        ),
        cost_estimate=pl.CostEstimate(
            flops=flops, transcendentals=heads_here * rows * span, bytes_accessed=bytes_accessed
        ),
        name="band_attention",
    )(q_doc.reshape(rows, 1), k_doc.reshape(1, keys), head_queries, head_upstream, head_keys)


def weight_kernel(me_ref, *refs, parts):
    pieces, grad_ref, out_ref = refs[:parts], refs[parts], refs[parts + 1]
    me = me_ref[0]
    total = None
    for shift in range(parts):
        source = lax.rem(me - shift + parts, parts)
        term = lax.dot_general(
            pieces[shift][...], grad_ref[source], (((0,), (0,)), ((), ())),
            preferred_element_type=jnp.float32,
        )
        total = term if total is None else total + term
    out_ref[...] = total.astype(out_ref.dtype)


def stacked_weight_product(me, pieces, grad_all):
    parts = len(pieces)
    rows, width = pieces[0].shape
    columns = grad_all.shape[2]
    tile = 512 if width % 512 == 0 else width
    grid_spec = pltpu.PrefetchScalarGridSpec(
        num_scalar_prefetch=1,
        grid=(width // tile,),
        in_specs=[pl.BlockSpec((rows, tile), lambda i, me: (0, i)) for _ in range(parts)]
        + [pl.BlockSpec((parts, rows, columns), lambda i, me: (0, 0, 0))],
        out_specs=pl.BlockSpec((tile, columns), lambda i, me: (i, 0)),
    )
    return pl.pallas_call(
        functools.partial(weight_kernel, parts=parts),
        grid_spec=grid_spec,
        out_shape=jax.ShapeDtypeStruct((width, columns), jnp.bfloat16),
        compiler_params=pltpu.CompilerParams(
            dimension_semantics=("arbitrary",), vmem_limit_bytes=48 * 1024 * 1024
        ),
        cost_estimate=pl.CostEstimate(
            flops=2 * parts * rows * width * columns,
            transcendentals=0,
            bytes_accessed=2 * parts * rows * (width + columns) + 2 * width * columns,
        ),
        name="weight_product",
    )(jnp.reshape(me, (1,)).astype(jnp.int32), *pieces, grad_all)


def send_hidden(hidden_rows):
    dp = lax.axis_size("dp")
    ctx = lax.axis_size("ctx")
    rows, features = hidden_rows.shape
    piece = features // (ctx * dp)
    width = features // dp
    me = lax.axis_index("dp")
    interleaved = hidden_rows.reshape(rows, ctx, dp, piece).transpose(2, 0, 1, 3).reshape(dp, rows, width)
    received = [lax.dynamic_index_in_dim(interleaved, me, 0, keepdims=False)]
    for shift in range(1, dp):
        outgoing = lax.dynamic_index_in_dim(interleaved, (me + shift) % dp, 0, keepdims=False)
        pairs = [(i, (i + shift) % dp) for i in range(dp)]
        received.append(lax.ppermute(outgoing, "dp", pairs))
    return me, received


def weight_gradient(me, received, grad_all):
    partial = stacked_weight_product(me, received, grad_all)
    reduced = lax.psum_scatter(partial, "ctx", scatter_dimension=0, tiled=True)
    return lax.all_to_all(reduced.astype(jnp.float32), "dp", split_axis=1, concat_axis=0, tiled=True)


def local_body(queries, kv_proj, hidden, grad_out, doc_lengths, slab_offsets):
    query_matrix_rows = queries[0]
    upstream_gradient = grad_out[0]
    key_matrix_rows = kv_proj[0]
    hidden_rows = hidden[0]
    bounds = jnp.cumsum(doc_lengths[0], dtype=jnp.int32)
    offset = slab_offsets[0]
    key_value_width = 2 * KEY_VALUE_HEADS * HEAD_FEATURES
    repeat_heads = lax.axis_size("ctx") // KEY_VALUE_HEADS
    key_total_count = key_matrix_rows.shape[0]
    copies = jnp.broadcast_to(
        key_matrix_rows.reshape(key_total_count, KEY_VALUE_HEADS, 1, 2 * HEAD_FEATURES),
        (key_total_count, KEY_VALUE_HEADS, repeat_heads, 2 * HEAD_FEATURES),
    ).reshape(key_total_count, KEY_VALUE_HEADS * repeat_heads * 2 * HEAD_FEATURES)
    head_queries, head_upstream, head_keys = (
        lax.all_to_all(query_matrix_rows, "ctx", split_axis=1, concat_axis=0, tiled=True),
        lax.all_to_all(upstream_gradient, "ctx", split_axis=1, concat_axis=0, tiled=True),
        lax.all_to_all(copies, "ctx", split_axis=1, concat_axis=0, tiled=True),
    )
    me, received = send_hidden(hidden_rows)
    rows = head_queries.shape[0]
    keys = head_keys.shape[0]
    query_pos = offset + jnp.arange(rows, dtype=jnp.int32)
    key_pos = offset - WINDOW + jnp.arange(keys, dtype=jnp.int32)
    q_doc = doc_index(query_pos, bounds)
    k_doc = jnp.where(key_pos >= 0, doc_index(key_pos, bounds), -1)
    attended_heads, grad_query_heads, grad_head = head_attention(
        head_queries, head_upstream, head_keys, q_doc, k_doc
    )
    attended, grad_query = (
        lax.all_to_all(attended_heads, "ctx", split_axis=0, concat_axis=1, tiled=True),
        lax.all_to_all(grad_query_heads, "ctx", split_axis=0, concat_axis=1, tiled=True),
    )
    partial_sums = lax.all_to_all(
        grad_head.astype(jnp.bfloat16), "ctx", split_axis=0, concat_axis=1, tiled=True
    )
    grad_keys = jnp.sum(
        partial_sums.reshape(
            partial_sums.shape[0], KEY_VALUE_HEADS, repeat_heads, 2 * HEAD_FEATURES
        ).astype(jnp.float32),
        axis=2,
    ).reshape(partial_sums.shape[0], key_value_width)
    grad_low = grad_keys.astype(jnp.bfloat16)
    grad_all = lax.all_gather(grad_low, "dp", axis=0, tiled=False)
    attended, grad_query, grad_all = lax.optimization_barrier((attended, grad_query, grad_all))
    grad_weight = weight_gradient(me, received, grad_all)
    return (attended[None], grad_query[None], grad_low[None], grad_weight)


def solution(mesh):
    in_specs = (
        P("dp", "ctx", None),
        P("dp", "ctx", None),
        P("dp", "ctx", None),
        P("dp", "ctx", None),
        P("dp", None),
        P("dp"),
    )
    out_specs = (P("dp", "ctx", None), P("dp", "ctx", None), P("dp", "ctx", None), P("ctx", "dp"))
    return jax.shard_map(local_body, mesh=mesh, in_specs=in_specs, out_specs=out_specs, check_vma=False)
```

```python
import functools

import jax
import jax.numpy as jnp
from jax import lax
from jax.experimental import pallas as pl
from jax.experimental.pallas import tpu as pltpu
from jax.sharding import PartitionSpec as P


HEAD_FEATURES = 128
KEY_VALUE_HEADS = 4
WINDOW = 2048
BLOCK_QUERIES = 256
CTX_ROWS = 4


def doc_index(positions, bounds):
    return jnp.sum(
        (bounds[None, :] <= positions[:, None]).astype(jnp.int32), axis=1, dtype=jnp.int32
    )


def attention_kernel(qdoc_ref, kdoc_ref, q_ref, go_ref, kv_ref, att_ref, dq_ref, dkv_ref, *, bq, span):
    qb = pl.program_id(0)
    h = pl.program_id(1)
    f32 = jnp.float32
    bf16 = jnp.bfloat16
    factor = HEAD_FEATURES ** (-0.5)

    @pl.when((qb == 0) & (h == 0))
    def _():
        dkv_ref[...] = jnp.zeros_like(dkv_ref)

    start = pl.multiple_of(qb * bq, bq)
    k = kv_ref[pl.ds(start, span), 0:HEAD_FEATURES]
    v = kv_ref[pl.ds(start, span), HEAD_FEATURES : 2 * HEAD_FEATURES]
    q = q_ref[...]
    go = go_ref[...]
    nt = (((1,), (1,)), ((), ()))
    tn = (((0,), (0,)), ((), ()))
    scores = lax.dot_general(q, k, nt, preferred_element_type=f32) * factor
    row = lax.broadcasted_iota(jnp.int32, (bq, span), 0)
    col = lax.broadcasted_iota(jnp.int32, (bq, span), 1)
    same_doc = qdoc_ref[...] == kdoc_ref[:, pl.ds(start, span)]
    allowed = (col > row) & (col <= row + WINDOW) & same_doc
    scores = jnp.where(allowed, scores, -1e30)
    maxima = jnp.max(scores, axis=1, keepdims=True)
    raised = jnp.exp(scores - maxima)
    weights = raised * (1.0 / jnp.sum(raised, axis=1, keepdims=True))
    weights_low = weights.astype(bf16)
    att = jnp.dot(weights_low, v, preferred_element_type=f32).astype(bf16)
    att_ref[...] = att
    grad_probs = lax.dot_general(go, v, nt, preferred_element_type=f32)
    deltas = jnp.sum(go.astype(f32) * att.astype(f32), axis=1, keepdims=True)
    grad_scores = (weights * (grad_probs - deltas) * factor).astype(bf16)
    dq_ref[...] = jnp.dot(grad_scores, k, preferred_element_type=f32).astype(bf16)
    dk = lax.dot_general(grad_scores, q, tn, preferred_element_type=f32)
    dv = lax.dot_general(weights_low, go, tn, preferred_element_type=f32)
    dkv_ref[pl.ds(start, span), 0:HEAD_FEATURES] += dk
    dkv_ref[pl.ds(start, span), HEAD_FEATURES : 2 * HEAD_FEATURES] += dv


def head_attention(head_queries, head_upstream, head_keys, q_doc, k_doc):
    rows = head_queries.shape[0]
    keys = head_keys.shape[0]
    heads_here = head_queries.shape[1] // HEAD_FEATURES
    bq = min(BLOCK_QUERIES, rows)
    span = bq + WINDOW
    grid = (rows // bq, heads_here)
    kernel = functools.partial(attention_kernel, bq=bq, span=span)
    flops = 12 * heads_here * rows * span * HEAD_FEATURES
    bytes_accessed = 2 * (4 * rows * heads_here * HEAD_FEATURES + keys * 2 * HEAD_FEATURES) + 4 * keys * 2 * HEAD_FEATURES
    return pl.pallas_call(
        kernel,
        grid=grid,
        in_specs=[
            pl.BlockSpec((bq, 1), lambda i, h: (i, 0)),
            pl.BlockSpec((1, keys), lambda i, h: (0, 0)),
            pl.BlockSpec((bq, HEAD_FEATURES), lambda i, h: (i, h)),
            pl.BlockSpec((bq, HEAD_FEATURES), lambda i, h: (i, h)),
            pl.BlockSpec((keys, 2 * HEAD_FEATURES), lambda i, h: (0, 0)),
        ],
        out_specs=[
            pl.BlockSpec((bq, HEAD_FEATURES), lambda i, h: (i, h)),
            pl.BlockSpec((bq, HEAD_FEATURES), lambda i, h: (i, h)),
            pl.BlockSpec((keys, 2 * HEAD_FEATURES), lambda i, h: (0, 0)),
        ],
        out_shape=[
            jax.ShapeDtypeStruct(head_queries.shape, jnp.bfloat16),
            jax.ShapeDtypeStruct(head_queries.shape, jnp.bfloat16),
            jax.ShapeDtypeStruct((keys, 2 * HEAD_FEATURES), jnp.float32),
        ],
        compiler_params=pltpu.CompilerParams(
            dimension_semantics=("arbitrary", "arbitrary"), vmem_limit_bytes=60 * 1024 * 1024
        ),
        cost_estimate=pl.CostEstimate(
            flops=flops, transcendentals=heads_here * rows * span, bytes_accessed=bytes_accessed
        ),
        name="band_attention",
    )(q_doc.reshape(rows, 1), k_doc.reshape(1, keys), head_queries, head_upstream, head_keys)


def weight_kernel(me_ref, *refs, parts):
    pieces, grad_ref, out_ref = refs[:parts], refs[parts], refs[parts + 1]
    me = me_ref[0]
    total = None
    for shift in range(parts):
        source = lax.rem(me - shift + parts, parts)
        term = lax.dot_general(
            pieces[shift][...], grad_ref[source], (((0,), (0,)), ((), ())),
            preferred_element_type=jnp.float32,
        )
        total = term if total is None else total + term
    out_ref[...] = total.astype(out_ref.dtype)


def stacked_weight_product(me, pieces, grad_all):
    parts = len(pieces)
    rows, width = pieces[0].shape
    columns = grad_all.shape[2]
    tile = 512 if width % 512 == 0 else width
    grid_spec = pltpu.PrefetchScalarGridSpec(
        num_scalar_prefetch=1,
        grid=(width // tile,),
        in_specs=[pl.BlockSpec((rows, tile), lambda i, me: (0, i)) for _ in range(parts)]
        + [pl.BlockSpec((parts, rows, columns), lambda i, me: (0, 0, 0))],
        out_specs=pl.BlockSpec((tile, columns), lambda i, me: (i, 0)),
    )
    return pl.pallas_call(
        functools.partial(weight_kernel, parts=parts),
        grid_spec=grid_spec,
        out_shape=jax.ShapeDtypeStruct((width, columns), jnp.bfloat16),
        compiler_params=pltpu.CompilerParams(
            dimension_semantics=("arbitrary",), vmem_limit_bytes=48 * 1024 * 1024
        ),
        cost_estimate=pl.CostEstimate(
            flops=2 * parts * rows * width * columns,
            transcendentals=0,
            bytes_accessed=2 * parts * rows * (width + columns) + 2 * width * columns,
        ),
        name="weight_product",
    )(jnp.reshape(me, (1,)).astype(jnp.int32), *pieces, grad_all)


def send_hidden(hidden_rows):
    dp = lax.axis_size("dp")
    ctx = lax.axis_size("ctx")
    rows, features = hidden_rows.shape
    piece = features // (ctx * dp)
    width = features // dp
    me = lax.axis_index("dp")
    across = ctx // CTX_ROWS
    interleaved = (
        hidden_rows.reshape(rows, CTX_ROWS, across, dp, piece)
        .transpose(3, 0, 2, 1, 4)
        .reshape(dp, rows, width)
    )
    received = [lax.dynamic_index_in_dim(interleaved, me, 0, keepdims=False)]
    for shift in range(1, dp):
        outgoing = lax.dynamic_index_in_dim(interleaved, (me + shift) % dp, 0, keepdims=False)
        pairs = [(i, (i + shift) % dp) for i in range(dp)]
        received.append(lax.ppermute(outgoing, "dp", pairs))
    return me, received


def weight_gradient(me, received, grad_all):
    partial = stacked_weight_product(me, received, grad_all)
    ctx = lax.axis_size("ctx")
    across = ctx // CTX_ROWS
    along_x = [[y * across + x for x in range(across)] for y in range(CTX_ROWS)]
    along_y = [[y * across + x for y in range(CTX_ROWS)] for x in range(across)]
    reduced = lax.psum_scatter(partial, "ctx", scatter_dimension=0, axis_index_groups=along_x, tiled=True)
    reduced = lax.psum_scatter(reduced, "ctx", scatter_dimension=0, axis_index_groups=along_y, tiled=True)
    return lax.all_to_all(reduced.astype(jnp.float32), "dp", split_axis=1, concat_axis=0, tiled=True)


def local_body(queries, kv_proj, hidden, grad_out, doc_lengths, slab_offsets):
    query_matrix_rows = queries[0]
    upstream_gradient = grad_out[0]
    key_matrix_rows = kv_proj[0]
    hidden_rows = hidden[0]
    bounds = jnp.cumsum(doc_lengths[0], dtype=jnp.int32)
    offset = slab_offsets[0]
    key_value_width = 2 * KEY_VALUE_HEADS * HEAD_FEATURES
    repeat_heads = lax.axis_size("ctx") // KEY_VALUE_HEADS
    key_total_count = key_matrix_rows.shape[0]
    copies = jnp.broadcast_to(
        key_matrix_rows.reshape(key_total_count, KEY_VALUE_HEADS, 1, 2 * HEAD_FEATURES),
        (key_total_count, KEY_VALUE_HEADS, repeat_heads, 2 * HEAD_FEATURES),
    ).reshape(key_total_count, KEY_VALUE_HEADS * repeat_heads * 2 * HEAD_FEATURES)
    head_queries, head_upstream, head_keys = (
        lax.all_to_all(query_matrix_rows, "ctx", split_axis=1, concat_axis=0, tiled=True),
        lax.all_to_all(upstream_gradient, "ctx", split_axis=1, concat_axis=0, tiled=True),
        lax.all_to_all(copies, "ctx", split_axis=1, concat_axis=0, tiled=True),
    )
    me, received = send_hidden(hidden_rows)
    rows = head_queries.shape[0]
    keys = head_keys.shape[0]
    query_pos = offset + jnp.arange(rows, dtype=jnp.int32)
    key_pos = offset - WINDOW + jnp.arange(keys, dtype=jnp.int32)
    q_doc = doc_index(query_pos, bounds)
    k_doc = jnp.where(key_pos >= 0, doc_index(key_pos, bounds), -1)
    attended_heads, grad_query_heads, grad_head = head_attention(head_queries, head_upstream, head_keys, q_doc, k_doc)
    attended, grad_query = (
        lax.all_to_all(attended_heads, "ctx", split_axis=0, concat_axis=1, tiled=True),
        lax.all_to_all(grad_query_heads, "ctx", split_axis=0, concat_axis=1, tiled=True),
    )
    partial_sums = lax.all_to_all(
        grad_head.astype(jnp.bfloat16), "ctx", split_axis=0, concat_axis=1, tiled=True
    )
    grad_keys = jnp.sum(
        partial_sums.reshape(
            partial_sums.shape[0], KEY_VALUE_HEADS, repeat_heads, 2 * HEAD_FEATURES
        ).astype(jnp.float32),
        axis=2,
    ).reshape(partial_sums.shape[0], key_value_width)
    grad_low = grad_keys.astype(jnp.bfloat16)
    grad_all = lax.all_gather(grad_low, "dp", axis=0, tiled=False)
    attended, grad_query, grad_all = lax.optimization_barrier((attended, grad_query, grad_all))
    grad_weight = weight_gradient(me, received, grad_all)
    return (attended[None], grad_query[None], grad_low[None], grad_weight)


def solution(mesh):
    in_specs = (
        P("dp", "ctx", None),
        P("dp", "ctx", None),
        P("dp", "ctx", None),
        P("dp", "ctx", None),
        P("dp", None),
        P("dp"),
    )
    out_specs = (P("dp", "ctx", None), P("dp", "ctx", None), P("dp", "ctx", None), P("ctx", "dp"))
    return jax.shard_map(local_body, mesh=mesh, in_specs=in_specs, out_specs=out_specs, check_vma=False)
```

```python
import functools

import jax
import jax.numpy as jnp
from jax import lax
from jax.experimental import pallas as pl
from jax.experimental.pallas import tpu as pltpu
from jax.sharding import PartitionSpec as P


HEAD_FEATURES = 128
KEY_VALUE_HEADS = 4
WINDOW = 2048
BLOCK_QUERIES = 256
CTX_ROWS = 4


def doc_index(positions, bounds):
    return jnp.sum(
        (bounds[None, :] <= positions[:, None]).astype(jnp.int32), axis=1, dtype=jnp.int32
    )


def attention_kernel(qdoc_ref, kdoc_ref, q_ref, go_ref, kv_ref, att_ref, dq_ref, dkv_ref, *, bq, span):
    qb = pl.program_id(0)
    h = pl.program_id(1)
    f32 = jnp.float32
    bf16 = jnp.bfloat16
    factor = HEAD_FEATURES ** (-0.5)

    @pl.when((qb == 0) & (h == 0))
    def _():
        dkv_ref[...] = jnp.zeros_like(dkv_ref)

    start = pl.multiple_of(qb * bq, bq)
    k = kv_ref[pl.ds(start, span), 0:HEAD_FEATURES]
    v = kv_ref[pl.ds(start, span), HEAD_FEATURES : 2 * HEAD_FEATURES]
    q = q_ref[...]
    go = go_ref[...]
    nt = (((1,), (1,)), ((), ()))
    tn = (((0,), (0,)), ((), ()))
    scores = lax.dot_general(q, k, nt, preferred_element_type=f32) * factor
    row = lax.broadcasted_iota(jnp.int32, (bq, span), 0)
    col = lax.broadcasted_iota(jnp.int32, (bq, span), 1)
    same_doc = qdoc_ref[...] == kdoc_ref[:, pl.ds(start, span)]
    allowed = (col > row) & (col <= row + WINDOW) & same_doc
    scores = jnp.where(allowed, scores, -1e30)
    maxima = jnp.max(scores, axis=1, keepdims=True)
    raised = jnp.exp(scores - maxima)
    weights = raised * (1.0 / jnp.sum(raised, axis=1, keepdims=True))
    weights_low = weights.astype(bf16)
    att = jnp.dot(weights_low, v, preferred_element_type=f32).astype(bf16)
    att_ref[...] = att
    grad_probs = lax.dot_general(go, v, nt, preferred_element_type=f32)
    deltas = jnp.sum(go.astype(f32) * att.astype(f32), axis=1, keepdims=True)
    grad_scores = (weights * (grad_probs - deltas) * factor).astype(bf16)
    dq_ref[...] = jnp.dot(grad_scores, k, preferred_element_type=f32).astype(bf16)
    dk = lax.dot_general(grad_scores, q, tn, preferred_element_type=f32)
    dv = lax.dot_general(weights_low, go, tn, preferred_element_type=f32)
    dkv_ref[pl.ds(start, span), 0:HEAD_FEATURES] += dk
    dkv_ref[pl.ds(start, span), HEAD_FEATURES : 2 * HEAD_FEATURES] += dv


def head_attention(head_queries, head_upstream, head_keys, q_doc, k_doc):
    rows = head_queries.shape[0]
    keys = head_keys.shape[0]
    heads_here = head_queries.shape[1] // HEAD_FEATURES
    bq = min(BLOCK_QUERIES, rows)
    span = bq + WINDOW
    grid = (rows // bq, heads_here)
    kernel = functools.partial(attention_kernel, bq=bq, span=span)
    flops = 12 * heads_here * rows * span * HEAD_FEATURES
    bytes_accessed = 2 * (4 * rows * heads_here * HEAD_FEATURES + keys * 2 * HEAD_FEATURES) + 4 * keys * 2 * HEAD_FEATURES
    return pl.pallas_call(
        kernel,
        grid=grid,
        in_specs=[
            pl.BlockSpec((bq, 1), lambda i, h: (i, 0)),
            pl.BlockSpec((1, keys), lambda i, h: (0, 0)),
            pl.BlockSpec((bq, HEAD_FEATURES), lambda i, h: (i, h)),
            pl.BlockSpec((bq, HEAD_FEATURES), lambda i, h: (i, h)),
            pl.BlockSpec((keys, 2 * HEAD_FEATURES), lambda i, h: (0, 0)),
        ],
        out_specs=[
            pl.BlockSpec((bq, HEAD_FEATURES), lambda i, h: (i, h)),
            pl.BlockSpec((bq, HEAD_FEATURES), lambda i, h: (i, h)),
            pl.BlockSpec((keys, 2 * HEAD_FEATURES), lambda i, h: (0, 0)),
        ],
        out_shape=[
            jax.ShapeDtypeStruct(head_queries.shape, jnp.bfloat16),
            jax.ShapeDtypeStruct(head_queries.shape, jnp.bfloat16),
            jax.ShapeDtypeStruct((keys, 2 * HEAD_FEATURES), jnp.float32),
        ],
        compiler_params=pltpu.CompilerParams(
            dimension_semantics=("arbitrary", "arbitrary"), vmem_limit_bytes=60 * 1024 * 1024
        ),
        cost_estimate=pl.CostEstimate(
            flops=flops, transcendentals=heads_here * rows * span, bytes_accessed=bytes_accessed
        ),
        name="band_attention",
    )(q_doc.reshape(rows, 1), k_doc.reshape(1, keys), head_queries, head_upstream, head_keys)


def weight_kernel(me_ref, *refs, parts):
    pieces, grad_ref, out_ref = refs[:parts], refs[parts], refs[parts + 1]
    me = me_ref[0]
    total = None
    for shift in range(parts):
        source = lax.rem(me - shift + parts, parts)
        term = lax.dot_general(
            pieces[shift][...], grad_ref[source], (((0,), (0,)), ((), ())),
            preferred_element_type=jnp.float32,
        )
        total = term if total is None else total + term
    out_ref[...] = total.astype(out_ref.dtype)


def stacked_weight_product(me, pieces, grad_all):
    parts = len(pieces)
    rows, width = pieces[0].shape
    columns = grad_all.shape[2]
    tile = 512 if width % 512 == 0 else width
    grid_spec = pltpu.PrefetchScalarGridSpec(
        num_scalar_prefetch=1,
        grid=(width // tile,),
        in_specs=[pl.BlockSpec((rows, tile), lambda i, me: (0, i)) for _ in range(parts)]
        + [pl.BlockSpec((parts, rows, columns), lambda i, me: (0, 0, 0))],
        out_specs=pl.BlockSpec((tile, columns), lambda i, me: (i, 0)),
    )
    return pl.pallas_call(
        functools.partial(weight_kernel, parts=parts),
        grid_spec=grid_spec,
        out_shape=jax.ShapeDtypeStruct((width, columns), jnp.bfloat16),
        compiler_params=pltpu.CompilerParams(
            dimension_semantics=("arbitrary",), vmem_limit_bytes=48 * 1024 * 1024
        ),
        cost_estimate=pl.CostEstimate(
            flops=2 * parts * rows * width * columns,
            transcendentals=0,
            bytes_accessed=2 * parts * rows * (width + columns) + 2 * width * columns,
        ),
        name="weight_product",
    )(jnp.reshape(me, (1,)).astype(jnp.int32), *pieces, grad_all)


def ctx_groups():
    ctx = lax.axis_size("ctx")
    across = ctx // CTX_ROWS
    along_x = [[y * across + x for x in range(across)] for y in range(CTX_ROWS)]
    along_y = [[y * across + x for y in range(CTX_ROWS)] for x in range(across)]
    return across, along_x, along_y


def gather_key_gradient(grad_head):
    keys, width = grad_head.shape
    across, along_x, along_y = ctx_groups()
    block = keys // (CTX_ROWS * across)
    ordered = (
        grad_head.astype(jnp.bfloat16)
        .reshape(CTX_ROWS, across, block, width)
        .transpose(1, 0, 2, 3)
        .reshape(keys, width)
    )
    summed = lax.psum_scatter(ordered, "ctx", scatter_dimension=0, axis_index_groups=along_x, tiled=True)
    owners = lax.all_to_all(
        summed.reshape(CTX_ROWS, block, width), "ctx", 0, 0, axis_index_groups=along_y, tiled=True
    )
    return owners.transpose(1, 0, 2).reshape(block, CTX_ROWS * width)


def send_hidden(hidden_rows):
    dp = lax.axis_size("dp")
    ctx = lax.axis_size("ctx")
    rows, features = hidden_rows.shape
    piece = features // (ctx * dp)
    width = features // dp
    me = lax.axis_index("dp")
    across = ctx // CTX_ROWS
    interleaved = (
        hidden_rows.reshape(rows, CTX_ROWS, across, dp, piece)
        .transpose(3, 0, 2, 1, 4)
        .reshape(dp, rows, width)
    )
    received = [lax.dynamic_index_in_dim(interleaved, me, 0, keepdims=False)]
    for shift in range(1, dp):
        outgoing = lax.dynamic_index_in_dim(interleaved, (me + shift) % dp, 0, keepdims=False)
        pairs = [(i, (i + shift) % dp) for i in range(dp)]
        received.append(lax.ppermute(outgoing, "dp", pairs))
    return me, received


def weight_gradient(me, received, grad_all):
    partial = stacked_weight_product(me, received, grad_all)
    _, along_x, along_y = ctx_groups()
    reduced = lax.psum_scatter(partial, "ctx", scatter_dimension=0, axis_index_groups=along_x, tiled=True)
    reduced = lax.psum_scatter(reduced, "ctx", scatter_dimension=0, axis_index_groups=along_y, tiled=True)
    return lax.all_to_all(reduced.astype(jnp.float32), "dp", split_axis=1, concat_axis=0, tiled=True)


def local_body(queries, kv_proj, hidden, grad_out, doc_lengths, slab_offsets):
    query_matrix_rows = queries[0]
    upstream_gradient = grad_out[0]
    key_matrix_rows = kv_proj[0]
    hidden_rows = hidden[0]
    bounds = jnp.cumsum(doc_lengths[0], dtype=jnp.int32)
    offset = slab_offsets[0]
    repeat_heads = lax.axis_size("ctx") // KEY_VALUE_HEADS
    key_total_count = key_matrix_rows.shape[0]
    copies = jnp.broadcast_to(
        key_matrix_rows.reshape(key_total_count, KEY_VALUE_HEADS, 1, 2 * HEAD_FEATURES),
        (key_total_count, KEY_VALUE_HEADS, repeat_heads, 2 * HEAD_FEATURES),
    ).reshape(key_total_count, KEY_VALUE_HEADS * repeat_heads * 2 * HEAD_FEATURES)
    head_queries, head_upstream, head_keys = (
        lax.all_to_all(query_matrix_rows, "ctx", split_axis=1, concat_axis=0, tiled=True),
        lax.all_to_all(upstream_gradient, "ctx", split_axis=1, concat_axis=0, tiled=True),
        lax.all_to_all(copies, "ctx", split_axis=1, concat_axis=0, tiled=True),
    )
    me, received = send_hidden(hidden_rows)
    rows = head_queries.shape[0]
    keys = head_keys.shape[0]
    query_pos = offset + jnp.arange(rows, dtype=jnp.int32)
    key_pos = offset - WINDOW + jnp.arange(keys, dtype=jnp.int32)
    q_doc = doc_index(query_pos, bounds)
    k_doc = jnp.where(key_pos >= 0, doc_index(key_pos, bounds), -1)
    attended_heads, grad_query_heads, grad_head = head_attention(head_queries, head_upstream, head_keys, q_doc, k_doc)
    attended, grad_query = (
        lax.all_to_all(attended_heads, "ctx", split_axis=0, concat_axis=1, tiled=True),
        lax.all_to_all(grad_query_heads, "ctx", split_axis=0, concat_axis=1, tiled=True),
    )
    grad_low = gather_key_gradient(grad_head)
    grad_all = lax.all_gather(grad_low, "dp", axis=0, tiled=False)
    attended, grad_query, grad_all = lax.optimization_barrier((attended, grad_query, grad_all))
    grad_weight = weight_gradient(me, received, grad_all)
    return (attended[None], grad_query[None], grad_low[None], grad_weight)


def solution(mesh):
    in_specs = (
        P("dp", "ctx", None),
        P("dp", "ctx", None),
        P("dp", "ctx", None),
        P("dp", "ctx", None),
        P("dp", None),
        P("dp"),
    )
    out_specs = (P("dp", "ctx", None), P("dp", "ctx", None), P("dp", "ctx", None), P("ctx", "dp"))
    return jax.shard_map(local_body, mesh=mesh, in_specs=in_specs, out_specs=out_specs, check_vma=False)
```

```python
import functools

import jax
import jax.numpy as jnp
from jax import lax
from jax.experimental import pallas as pl
from jax.experimental.pallas import tpu as pltpu
from jax.sharding import PartitionSpec as P


HEAD_FEATURES = 128
KEY_VALUE_HEADS = 4
WINDOW = 2048
BLOCK_QUERIES = 256
CTX_ROWS = 4


def doc_index(positions, bounds):
    return jnp.sum(
        (bounds[None, :] <= positions[:, None]).astype(jnp.int32), axis=1, dtype=jnp.int32
    )


def attention_kernel(qdoc_ref, kdoc_ref, q_ref, go_ref, kv_ref, att_ref, dq_ref, dkv_ref, *, bq, span):
    qb = pl.program_id(0)
    h = pl.program_id(1)
    f32 = jnp.float32
    bf16 = jnp.bfloat16
    factor = HEAD_FEATURES ** (-0.5)

    @pl.when((qb == 0) & (h == 0))
    def _():
        dkv_ref[...] = jnp.zeros_like(dkv_ref)

    start = pl.multiple_of(qb * bq, bq)
    k = kv_ref[pl.ds(start, span), 0:HEAD_FEATURES]
    v = kv_ref[pl.ds(start, span), HEAD_FEATURES : 2 * HEAD_FEATURES]
    q = q_ref[...]
    go = go_ref[...]
    nt = (((1,), (1,)), ((), ()))
    tn = (((0,), (0,)), ((), ()))
    scores = lax.dot_general(q, k, nt, preferred_element_type=f32) * factor
    row = lax.broadcasted_iota(jnp.int32, (bq, span), 0)
    col = lax.broadcasted_iota(jnp.int32, (bq, span), 1)
    same_doc = qdoc_ref[...] == kdoc_ref[:, pl.ds(start, span)]
    allowed = (col > row) & (col <= row + WINDOW) & same_doc
    scores = jnp.where(allowed, scores, -1e30)
    maxima = jnp.max(scores, axis=1, keepdims=True)
    raised = jnp.exp(scores - maxima)
    weights = raised * (1.0 / jnp.sum(raised, axis=1, keepdims=True))
    weights_low = weights.astype(bf16)
    att = jnp.dot(weights_low, v, preferred_element_type=f32).astype(bf16)
    att_ref[...] = att
    grad_probs = lax.dot_general(go, v, nt, preferred_element_type=f32)
    deltas = jnp.sum(go.astype(f32) * att.astype(f32), axis=1, keepdims=True)
    grad_scores = (weights * (grad_probs - deltas) * factor).astype(bf16)
    dq_ref[...] = jnp.dot(grad_scores, k, preferred_element_type=f32).astype(bf16)
    dk = lax.dot_general(q, grad_scores, tn, preferred_element_type=f32)
    dv = lax.dot_general(go, weights_low, tn, preferred_element_type=f32)
    dkv_ref[0:HEAD_FEATURES, pl.ds(start, span)] += dk
    dkv_ref[HEAD_FEATURES : 2 * HEAD_FEATURES, pl.ds(start, span)] += dv


def head_attention(head_queries, head_upstream, head_keys, q_doc, k_doc):
    rows = head_queries.shape[0]
    keys = head_keys.shape[0]
    heads_here = head_queries.shape[1] // HEAD_FEATURES
    bq = min(BLOCK_QUERIES, rows)
    span = bq + WINDOW
    grid = (rows // bq, heads_here)
    kernel = functools.partial(attention_kernel, bq=bq, span=span)
    flops = 12 * heads_here * rows * span * HEAD_FEATURES
    bytes_accessed = 2 * (4 * rows * heads_here * HEAD_FEATURES + keys * 2 * HEAD_FEATURES) + 4 * keys * 2 * HEAD_FEATURES
    return pl.pallas_call(
        kernel,
        grid=grid,
        in_specs=[
            pl.BlockSpec((bq, 1), lambda i, h: (i, 0)),
            pl.BlockSpec((1, keys), lambda i, h: (0, 0)),
            pl.BlockSpec((bq, HEAD_FEATURES), lambda i, h: (i, h)),
            pl.BlockSpec((bq, HEAD_FEATURES), lambda i, h: (i, h)),
            pl.BlockSpec((keys, 2 * HEAD_FEATURES), lambda i, h: (0, 0)),
        ],
        out_specs=[
            pl.BlockSpec((bq, HEAD_FEATURES), lambda i, h: (i, h)),
            pl.BlockSpec((bq, HEAD_FEATURES), lambda i, h: (i, h)),
            pl.BlockSpec((2 * HEAD_FEATURES, keys), lambda i, h: (0, 0)),
        ],
        out_shape=[
            jax.ShapeDtypeStruct(head_queries.shape, jnp.bfloat16),
            jax.ShapeDtypeStruct(head_queries.shape, jnp.bfloat16),
            jax.ShapeDtypeStruct((2 * HEAD_FEATURES, keys), jnp.float32),
        ],
        compiler_params=pltpu.CompilerParams(
            dimension_semantics=("arbitrary", "arbitrary"), vmem_limit_bytes=60 * 1024 * 1024
        ),
        cost_estimate=pl.CostEstimate(
            flops=flops, transcendentals=heads_here * rows * span, bytes_accessed=bytes_accessed
        ),
        name="band_attention",
    )(q_doc.reshape(rows, 1), k_doc.reshape(1, keys), head_queries, head_upstream, head_keys)


def weight_kernel(me_ref, *refs, parts):
    pieces, grad_ref, out_ref = refs[:parts], refs[parts], refs[parts + 1]
    me = me_ref[0]
    total = None
    for shift in range(parts):
        source = lax.rem(me - shift + parts, parts)
        term = lax.dot_general(
            pieces[shift][...], grad_ref[source], (((0,), (0,)), ((), ())),
            preferred_element_type=jnp.float32,
        )
        total = term if total is None else total + term
    out_ref[...] = total.astype(out_ref.dtype)


def stacked_weight_product(me, pieces, grad_all):
    parts = len(pieces)
    rows, width = pieces[0].shape
    columns = grad_all.shape[2]
    tile = 512 if width % 512 == 0 else width
    grid_spec = pltpu.PrefetchScalarGridSpec(
        num_scalar_prefetch=1,
        grid=(width // tile,),
        in_specs=[pl.BlockSpec((rows, tile), lambda i, me: (0, i)) for _ in range(parts)]
        + [pl.BlockSpec((parts, rows, columns), lambda i, me: (0, 0, 0))],
        out_specs=pl.BlockSpec((tile, columns), lambda i, me: (i, 0)),
    )
    return pl.pallas_call(
        functools.partial(weight_kernel, parts=parts),
        grid_spec=grid_spec,
        out_shape=jax.ShapeDtypeStruct((width, columns), jnp.bfloat16),
        compiler_params=pltpu.CompilerParams(
            dimension_semantics=("arbitrary",), vmem_limit_bytes=48 * 1024 * 1024
        ),
        cost_estimate=pl.CostEstimate(
            flops=2 * parts * rows * width * columns,
            transcendentals=0,
            bytes_accessed=2 * parts * rows * (width + columns) + 2 * width * columns,
        ),
        name="weight_product",
    )(jnp.reshape(me, (1,)).astype(jnp.int32), *pieces, grad_all)


def send_hidden(hidden_rows):
    dp = lax.axis_size("dp")
    ctx = lax.axis_size("ctx")
    rows, features = hidden_rows.shape
    piece = features // (ctx * dp)
    width = features // dp
    me = lax.axis_index("dp")
    across = ctx // CTX_ROWS
    interleaved = (
        hidden_rows.reshape(rows, CTX_ROWS, across, dp, piece)
        .transpose(3, 0, 2, 1, 4)
        .reshape(dp, rows, width)
    )
    received = [lax.dynamic_index_in_dim(interleaved, me, 0, keepdims=False)]
    for shift in range(1, dp):
        outgoing = lax.dynamic_index_in_dim(interleaved, (me + shift) % dp, 0, keepdims=False)
        pairs = [(i, (i + shift) % dp) for i in range(dp)]
        received.append(lax.ppermute(outgoing, "dp", pairs))
    return me, received


def weight_gradient(me, received, grad_all):
    partial = stacked_weight_product(me, received, grad_all)
    ctx = lax.axis_size("ctx")
    across = ctx // CTX_ROWS
    along_x = [[y * across + x for x in range(across)] for y in range(CTX_ROWS)]
    along_y = [[y * across + x for y in range(CTX_ROWS)] for x in range(across)]
    reduced = lax.psum_scatter(partial, "ctx", scatter_dimension=0, axis_index_groups=along_x, tiled=True)
    reduced = lax.psum_scatter(reduced, "ctx", scatter_dimension=0, axis_index_groups=along_y, tiled=True)
    return lax.all_to_all(reduced.astype(jnp.float32), "dp", split_axis=1, concat_axis=0, tiled=True)


def local_body(queries, kv_proj, hidden, grad_out, doc_lengths, slab_offsets):
    query_matrix_rows = queries[0]
    upstream_gradient = grad_out[0]
    key_matrix_rows = kv_proj[0]
    hidden_rows = hidden[0]
    bounds = jnp.cumsum(doc_lengths[0], dtype=jnp.int32)
    offset = slab_offsets[0]
    key_value_width = 2 * KEY_VALUE_HEADS * HEAD_FEATURES
    repeat_heads = lax.axis_size("ctx") // KEY_VALUE_HEADS
    key_total_count = key_matrix_rows.shape[0]
    copies = jnp.broadcast_to(
        key_matrix_rows.reshape(key_total_count, KEY_VALUE_HEADS, 1, 2 * HEAD_FEATURES),
        (key_total_count, KEY_VALUE_HEADS, repeat_heads, 2 * HEAD_FEATURES),
    ).reshape(key_total_count, KEY_VALUE_HEADS * repeat_heads * 2 * HEAD_FEATURES)
    head_queries, head_upstream, head_keys = (
        lax.all_to_all(query_matrix_rows, "ctx", split_axis=1, concat_axis=0, tiled=True),
        lax.all_to_all(upstream_gradient, "ctx", split_axis=1, concat_axis=0, tiled=True),
        lax.all_to_all(copies, "ctx", split_axis=1, concat_axis=0, tiled=True),
    )
    me, received = send_hidden(hidden_rows)
    rows = head_queries.shape[0]
    keys = head_keys.shape[0]
    query_pos = offset + jnp.arange(rows, dtype=jnp.int32)
    key_pos = offset - WINDOW + jnp.arange(keys, dtype=jnp.int32)
    q_doc = doc_index(query_pos, bounds)
    k_doc = jnp.where(key_pos >= 0, doc_index(key_pos, bounds), -1)
    attended_heads, grad_query_heads, grad_head = head_attention(head_queries, head_upstream, head_keys, q_doc, k_doc)
    attended, grad_query = (
        lax.all_to_all(attended_heads, "ctx", split_axis=0, concat_axis=1, tiled=True),
        lax.all_to_all(grad_query_heads, "ctx", split_axis=0, concat_axis=1, tiled=True),
    )
    partial_sums = lax.all_to_all(
        grad_head.T.astype(jnp.bfloat16), "ctx", split_axis=0, concat_axis=1, tiled=True
    )
    grad_keys = jnp.sum(
        partial_sums.reshape(
            partial_sums.shape[0], KEY_VALUE_HEADS, repeat_heads, 2 * HEAD_FEATURES
        ).astype(jnp.float32),
        axis=2,
    ).reshape(partial_sums.shape[0], key_value_width)
    grad_low = grad_keys.astype(jnp.bfloat16)
    grad_all = lax.all_gather(grad_low, "dp", axis=0, tiled=False)
    attended, grad_query, grad_all = lax.optimization_barrier((attended, grad_query, grad_all))
    grad_weight = weight_gradient(me, received, grad_all)
    return (attended[None], grad_query[None], grad_low[None], grad_weight)


def solution(mesh):
    in_specs = (
        P("dp", "ctx", None),
        P("dp", "ctx", None),
        P("dp", "ctx", None),
        P("dp", "ctx", None),
        P("dp", None),
        P("dp"),
    )
    out_specs = (P("dp", "ctx", None), P("dp", "ctx", None), P("dp", "ctx", None), P("ctx", "dp"))
    return jax.shard_map(local_body, mesh=mesh, in_specs=in_specs, out_specs=out_specs, check_vma=False)
```

```python
import functools

import jax
import jax.numpy as jnp
from jax import lax
from jax.experimental import pallas as pl
from jax.experimental.pallas import tpu as pltpu
from jax.sharding import PartitionSpec as P


HEAD_FEATURES = 128
KEY_VALUE_HEADS = 4
WINDOW = 2048
BLOCK_QUERIES = 256
CTX_ROWS = 4


def doc_index(positions, bounds):
    return jnp.sum(
        (bounds[None, :] <= positions[:, None]).astype(jnp.int32), axis=1, dtype=jnp.int32
    )


def attention_kernel(qdoc_ref, kdoc_ref, q_ref, go_ref, kv_ref, att_ref, dq_ref, dkv_ref, *, bq, span):
    qb = pl.program_id(0)
    h = pl.program_id(1)
    f32 = jnp.float32
    bf16 = jnp.bfloat16
    factor = HEAD_FEATURES ** (-0.5)

    @pl.when((qb == 0) & (h == 0))
    def _():
        dkv_ref[...] = jnp.zeros_like(dkv_ref)

    start = pl.multiple_of(qb * bq, bq)
    k = kv_ref[pl.ds(start, span), 0:HEAD_FEATURES]
    v = kv_ref[pl.ds(start, span), HEAD_FEATURES : 2 * HEAD_FEATURES]
    q = q_ref[...]
    go = go_ref[...]
    nt = (((1,), (1,)), ((), ()))
    tn = (((0,), (0,)), ((), ()))
    scores = lax.dot_general(q, k, nt, preferred_element_type=f32) * factor
    row = lax.broadcasted_iota(jnp.int32, (bq, span), 0)
    col = lax.broadcasted_iota(jnp.int32, (bq, span), 1)
    same_doc = qdoc_ref[...] == kdoc_ref[:, pl.ds(start, span)]
    allowed = (col > row) & (col <= row + WINDOW) & same_doc
    scores = jnp.where(allowed, scores, -1e30)
    maxima = jnp.max(scores, axis=1, keepdims=True)
    raised = jnp.exp(scores - maxima)
    weights = raised * (1.0 / jnp.sum(raised, axis=1, keepdims=True))
    weights_low = weights.astype(bf16)
    att = jnp.dot(weights_low, v, preferred_element_type=f32).astype(bf16)
    att_ref[...] = att
    grad_probs = lax.dot_general(go, v, nt, preferred_element_type=f32)
    deltas = jnp.sum(go.astype(f32) * att.astype(f32), axis=1, keepdims=True)
    grad_scores = (weights * (grad_probs - deltas) * factor).astype(bf16)
    dq_ref[...] = jnp.dot(grad_scores, k, preferred_element_type=f32).astype(bf16)
    dk = lax.dot_general(q, grad_scores, tn, preferred_element_type=f32)
    dv = lax.dot_general(go, weights_low, tn, preferred_element_type=f32)
    dkv_ref[0:HEAD_FEATURES, pl.ds(start, span)] += dk
    dkv_ref[HEAD_FEATURES : 2 * HEAD_FEATURES, pl.ds(start, span)] += dv


def head_attention(head_queries, head_upstream, head_keys, q_doc, k_doc):
    rows = head_queries.shape[0]
    keys = head_keys.shape[0]
    heads_here = head_queries.shape[1] // HEAD_FEATURES
    bq = min(BLOCK_QUERIES, rows)
    span = bq + WINDOW
    grid = (rows // bq, heads_here)
    kernel = functools.partial(attention_kernel, bq=bq, span=span)
    flops = 12 * heads_here * rows * span * HEAD_FEATURES
    bytes_accessed = 2 * (4 * rows * heads_here * HEAD_FEATURES + keys * 2 * HEAD_FEATURES) + 4 * keys * 2 * HEAD_FEATURES
    return pl.pallas_call(
        kernel,
        grid=grid,
        in_specs=[
            pl.BlockSpec((bq, 1), lambda i, h: (i, 0)),
            pl.BlockSpec((1, keys), lambda i, h: (0, 0)),
            pl.BlockSpec((bq, HEAD_FEATURES), lambda i, h: (i, h)),
            pl.BlockSpec((bq, HEAD_FEATURES), lambda i, h: (i, h)),
            pl.BlockSpec((keys, 2 * HEAD_FEATURES), lambda i, h: (0, 0)),
        ],
        out_specs=[
            pl.BlockSpec((bq, HEAD_FEATURES), lambda i, h: (i, h)),
            pl.BlockSpec((bq, HEAD_FEATURES), lambda i, h: (i, h)),
            pl.BlockSpec((2 * HEAD_FEATURES, keys), lambda i, h: (0, 0)),
        ],
        out_shape=[
            jax.ShapeDtypeStruct(head_queries.shape, jnp.bfloat16),
            jax.ShapeDtypeStruct(head_queries.shape, jnp.bfloat16),
            jax.ShapeDtypeStruct((2 * HEAD_FEATURES, keys), jnp.float32),
        ],
        compiler_params=pltpu.CompilerParams(
            dimension_semantics=("arbitrary", "arbitrary"), vmem_limit_bytes=60 * 1024 * 1024
        ),
        cost_estimate=pl.CostEstimate(
            flops=flops, transcendentals=heads_here * rows * span, bytes_accessed=bytes_accessed
        ),
        name="band_attention",
    )(q_doc.reshape(rows, 1), k_doc.reshape(1, keys), head_queries, head_upstream, head_keys)


def weight_kernel(me_ref, *refs, parts):
    pieces, grad_ref, out_ref = refs[:parts], refs[parts], refs[parts + 1]
    me = me_ref[0]
    total = None
    for shift in range(parts):
        source = lax.rem(me - shift + parts, parts)
        term = lax.dot_general(
            pieces[shift][...], grad_ref[source], (((0,), (0,)), ((), ())),
            preferred_element_type=jnp.float32,
        )
        total = term if total is None else total + term
    out_ref[...] = total.astype(out_ref.dtype)


def stacked_weight_product(me, pieces, grad_all):
    parts = len(pieces)
    rows, width = pieces[0].shape
    columns = grad_all.shape[2]
    tile = 512 if width % 512 == 0 else width
    grid_spec = pltpu.PrefetchScalarGridSpec(
        num_scalar_prefetch=1,
        grid=(width // tile,),
        in_specs=[pl.BlockSpec((rows, tile), lambda i, me: (0, i)) for _ in range(parts)]
        + [pl.BlockSpec((parts, rows, columns), lambda i, me: (0, 0, 0))],
        out_specs=pl.BlockSpec((tile, columns), lambda i, me: (i, 0)),
    )
    return pl.pallas_call(
        functools.partial(weight_kernel, parts=parts),
        grid_spec=grid_spec,
        out_shape=jax.ShapeDtypeStruct((width, columns), jnp.bfloat16),
        compiler_params=pltpu.CompilerParams(
            dimension_semantics=("arbitrary",), vmem_limit_bytes=48 * 1024 * 1024
        ),
        cost_estimate=pl.CostEstimate(
            flops=2 * parts * rows * width * columns,
            transcendentals=0,
            bytes_accessed=2 * parts * rows * (width + columns) + 2 * width * columns,
        ),
        name="weight_product",
    )(jnp.reshape(me, (1,)).astype(jnp.int32), *pieces, grad_all)


def send_hidden(hidden_rows):
    dp = lax.axis_size("dp")
    ctx = lax.axis_size("ctx")
    rows, features = hidden_rows.shape
    piece = features // (ctx * dp)
    width = features // dp
    me = lax.axis_index("dp")
    across = ctx // CTX_ROWS
    interleaved = (
        hidden_rows.reshape(rows, CTX_ROWS, across, dp, piece)
        .transpose(3, 0, 2, 1, 4)
        .reshape(dp, rows, width)
    )
    received = [lax.dynamic_index_in_dim(interleaved, me, 0, keepdims=False)]
    for shift in range(1, dp):
        outgoing = lax.dynamic_index_in_dim(interleaved, (me + shift) % dp, 0, keepdims=False)
        pairs = [(i, (i + shift) % dp) for i in range(dp)]
        received.append(lax.ppermute(outgoing, "dp", pairs))
    return me, received


def weight_gradient(me, received, grad_all, grad_query_heads):
    partial = stacked_weight_product(me, received, grad_all)
    ctx = lax.axis_size("ctx")
    across = ctx // CTX_ROWS
    along_x = [[y * across + x for x in range(across)] for y in range(CTX_ROWS)]
    along_y = [[y * across + x for y in range(CTX_ROWS)] for x in range(across)]
    reduced = lax.psum_scatter(partial, "ctx", scatter_dimension=0, axis_index_groups=along_x, tiled=True)
    reduced, grad_query_heads = lax.optimization_barrier((reduced, grad_query_heads))
    grad_query = lax.all_to_all(grad_query_heads, "ctx", split_axis=0, concat_axis=1, tiled=True)
    reduced = lax.psum_scatter(reduced, "ctx", scatter_dimension=0, axis_index_groups=along_y, tiled=True)
    weight = lax.all_to_all(reduced.astype(jnp.float32), "dp", split_axis=1, concat_axis=0, tiled=True)
    return weight, grad_query


def local_body(queries, kv_proj, hidden, grad_out, doc_lengths, slab_offsets):
    query_matrix_rows = queries[0]
    upstream_gradient = grad_out[0]
    key_matrix_rows = kv_proj[0]
    hidden_rows = hidden[0]
    bounds = jnp.cumsum(doc_lengths[0], dtype=jnp.int32)
    offset = slab_offsets[0]
    key_value_width = 2 * KEY_VALUE_HEADS * HEAD_FEATURES
    repeat_heads = lax.axis_size("ctx") // KEY_VALUE_HEADS
    key_total_count = key_matrix_rows.shape[0]
    copies = jnp.broadcast_to(
        key_matrix_rows.reshape(key_total_count, KEY_VALUE_HEADS, 1, 2 * HEAD_FEATURES),
        (key_total_count, KEY_VALUE_HEADS, repeat_heads, 2 * HEAD_FEATURES),
    ).reshape(key_total_count, KEY_VALUE_HEADS * repeat_heads * 2 * HEAD_FEATURES)
    head_queries, head_upstream, head_keys = (
        lax.all_to_all(query_matrix_rows, "ctx", split_axis=1, concat_axis=0, tiled=True),
        lax.all_to_all(upstream_gradient, "ctx", split_axis=1, concat_axis=0, tiled=True),
        lax.all_to_all(copies, "ctx", split_axis=1, concat_axis=0, tiled=True),
    )
    me, received = send_hidden(hidden_rows)
    rows = head_queries.shape[0]
    keys = head_keys.shape[0]
    query_pos = offset + jnp.arange(rows, dtype=jnp.int32)
    key_pos = offset - WINDOW + jnp.arange(keys, dtype=jnp.int32)
    q_doc = doc_index(query_pos, bounds)
    k_doc = jnp.where(key_pos >= 0, doc_index(key_pos, bounds), -1)
    attended_heads, grad_query_heads, grad_head = head_attention(head_queries, head_upstream, head_keys, q_doc, k_doc)
    attended = lax.all_to_all(attended_heads, "ctx", split_axis=0, concat_axis=1, tiled=True)
    partial_sums = lax.all_to_all(
        grad_head.T.astype(jnp.bfloat16), "ctx", split_axis=0, concat_axis=1, tiled=True
    )
    grad_keys = jnp.sum(
        partial_sums.reshape(
            partial_sums.shape[0], KEY_VALUE_HEADS, repeat_heads, 2 * HEAD_FEATURES
        ).astype(jnp.float32),
        axis=2,
    ).reshape(partial_sums.shape[0], key_value_width)
    grad_low = grad_keys.astype(jnp.bfloat16)
    grad_all = lax.all_gather(grad_low, "dp", axis=0, tiled=False)
    attended, grad_all = lax.optimization_barrier((attended, grad_all))
    grad_weight, grad_query = weight_gradient(me, received, grad_all, grad_query_heads)
    return (attended[None], grad_query[None], grad_low[None], grad_weight)


def solution(mesh):
    in_specs = (
        P("dp", "ctx", None),
        P("dp", "ctx", None),
        P("dp", "ctx", None),
        P("dp", "ctx", None),
        P("dp", None),
        P("dp"),
    )
    out_specs = (P("dp", "ctx", None), P("dp", "ctx", None), P("dp", "ctx", None), P("ctx", "dp"))
    return jax.shard_map(local_body, mesh=mesh, in_specs=in_specs, out_specs=out_specs, check_vma=False)
```

```python
import functools

import jax
import jax.numpy as jnp
from jax import lax
from jax.experimental import pallas as pl
from jax.experimental.pallas import tpu as pltpu
from jax.sharding import PartitionSpec as P


HEAD_FEATURES = 128
KEY_VALUE_HEADS = 4
WINDOW = 2048
BLOCK_QUERIES = 256
CTX_ROWS = 4


def doc_index(positions, bounds):
    return jnp.sum(
        (bounds[None, :] <= positions[:, None]).astype(jnp.int32), axis=1, dtype=jnp.int32
    )


def attention_kernel(qdoc_ref, kdoc_ref, q_ref, go_ref, kv_ref, att_ref, dq_ref, dkv_ref, *, bq, span, heads):
    qb = pl.program_id(0)
    f32 = jnp.float32
    bf16 = jnp.bfloat16
    factor = HEAD_FEATURES ** (-0.5)

    @pl.when(qb == 0)
    def _():
        dkv_ref[...] = jnp.zeros_like(dkv_ref)

    start = pl.multiple_of(qb * bq, bq)
    k = kv_ref[pl.ds(start, span), 0:HEAD_FEATURES]
    v = kv_ref[pl.ds(start, span), HEAD_FEATURES : 2 * HEAD_FEATURES]
    nt = (((1,), (1,)), ((), ()))
    tn = (((0,), (0,)), ((), ()))
    row = lax.broadcasted_iota(jnp.int32, (bq, span), 0)
    col = lax.broadcasted_iota(jnp.int32, (bq, span), 1)
    same_doc = qdoc_ref[...] == kdoc_ref[:, pl.ds(start, span)]
    allowed = (col > row) & (col <= row + WINDOW) & same_doc
    for h in range(heads):
        cols = slice(h * HEAD_FEATURES, (h + 1) * HEAD_FEATURES)
        q = q_ref[:, cols]
        go = go_ref[:, cols]
        scores = lax.dot_general(q, k, nt, preferred_element_type=f32) * factor
        scores = jnp.where(allowed, scores, -1e30)
        maxima = jnp.max(scores, axis=1, keepdims=True)
        raised = jnp.exp(scores - maxima)
        weights = raised * (1.0 / jnp.sum(raised, axis=1, keepdims=True))
        weights_low = weights.astype(bf16)
        att = jnp.dot(weights_low, v, preferred_element_type=f32).astype(bf16)
        att_ref[:, cols] = att
        grad_probs = lax.dot_general(go, v, nt, preferred_element_type=f32)
        deltas = jnp.sum(go.astype(f32) * att.astype(f32), axis=1, keepdims=True)
        grad_scores = (weights * (grad_probs - deltas) * factor).astype(bf16)
        dq_ref[:, cols] = jnp.dot(grad_scores, k, preferred_element_type=f32).astype(bf16)
        dk = lax.dot_general(q, grad_scores, tn, preferred_element_type=f32)
        dv = lax.dot_general(go, weights_low, tn, preferred_element_type=f32)
        dkv_ref[0:HEAD_FEATURES, pl.ds(start, span)] += dk
        dkv_ref[HEAD_FEATURES : 2 * HEAD_FEATURES, pl.ds(start, span)] += dv


def head_attention(head_queries, head_upstream, head_keys, q_doc, k_doc):
    rows = head_queries.shape[0]
    keys = head_keys.shape[0]
    heads_here = head_queries.shape[1] // HEAD_FEATURES
    bq = min(BLOCK_QUERIES, rows)
    span = bq + WINDOW
    grid = (rows // bq,)
    kernel = functools.partial(attention_kernel, bq=bq, span=span, heads=heads_here)
    width = heads_here * HEAD_FEATURES
    flops = 12 * heads_here * rows * span * HEAD_FEATURES
    bytes_accessed = 2 * (4 * rows * heads_here * HEAD_FEATURES + keys * 2 * HEAD_FEATURES) + 4 * keys * 2 * HEAD_FEATURES
    return pl.pallas_call(
        kernel,
        grid=grid,
        in_specs=[
            pl.BlockSpec((bq, 1), lambda i: (i, 0)),
            pl.BlockSpec((1, keys), lambda i: (0, 0)),
            pl.BlockSpec((bq, width), lambda i: (i, 0)),
            pl.BlockSpec((bq, width), lambda i: (i, 0)),
            pl.BlockSpec((keys, 2 * HEAD_FEATURES), lambda i: (0, 0)),
        ],
        out_specs=[
            pl.BlockSpec((bq, width), lambda i: (i, 0)),
            pl.BlockSpec((bq, width), lambda i: (i, 0)),
            pl.BlockSpec((2 * HEAD_FEATURES, keys), lambda i: (0, 0)),
        ],
        out_shape=[
            jax.ShapeDtypeStruct(head_queries.shape, jnp.bfloat16),
            jax.ShapeDtypeStruct(head_queries.shape, jnp.bfloat16),
            jax.ShapeDtypeStruct((2 * HEAD_FEATURES, keys), jnp.float32),
        ],
        compiler_params=pltpu.CompilerParams(
            dimension_semantics=("arbitrary",), vmem_limit_bytes=60 * 1024 * 1024
        ),
        cost_estimate=pl.CostEstimate(
            flops=flops, transcendentals=heads_here * rows * span, bytes_accessed=bytes_accessed
        ),
        name="band_attention",
    )(q_doc.reshape(rows, 1), k_doc.reshape(1, keys), head_queries, head_upstream, head_keys)


def weight_kernel(me_ref, *refs, parts):
    pieces, grad_ref, out_ref = refs[:parts], refs[parts], refs[parts + 1]
    me = me_ref[0]
    total = None
    for shift in range(parts):
        source = lax.rem(me - shift + parts, parts)
        term = lax.dot_general(
            pieces[shift][...], grad_ref[source], (((0,), (0,)), ((), ())),
            preferred_element_type=jnp.float32,
        )
        total = term if total is None else total + term
    out_ref[...] = total.astype(out_ref.dtype)


def stacked_weight_product(me, pieces, grad_all):
    parts = len(pieces)
    rows, width = pieces[0].shape
    columns = grad_all.shape[2]
    tile = 512 if width % 512 == 0 else width
    grid_spec = pltpu.PrefetchScalarGridSpec(
        num_scalar_prefetch=1,
        grid=(width // tile,),
        in_specs=[pl.BlockSpec((rows, tile), lambda i, me: (0, i)) for _ in range(parts)]
        + [pl.BlockSpec((parts, rows, columns), lambda i, me: (0, 0, 0))],
        out_specs=pl.BlockSpec((tile, columns), lambda i, me: (i, 0)),
    )
    return pl.pallas_call(
        functools.partial(weight_kernel, parts=parts),
        grid_spec=grid_spec,
        out_shape=jax.ShapeDtypeStruct((width, columns), jnp.bfloat16),
        compiler_params=pltpu.CompilerParams(
            dimension_semantics=("arbitrary",), vmem_limit_bytes=48 * 1024 * 1024
        ),
        cost_estimate=pl.CostEstimate(
            flops=2 * parts * rows * width * columns,
            transcendentals=0,
            bytes_accessed=2 * parts * rows * (width + columns) + 2 * width * columns,
        ),
        name="weight_product",
    )(jnp.reshape(me, (1,)).astype(jnp.int32), *pieces, grad_all)


def send_hidden(hidden_rows):
    dp = lax.axis_size("dp")
    ctx = lax.axis_size("ctx")
    rows, features = hidden_rows.shape
    piece = features // (ctx * dp)
    width = features // dp
    me = lax.axis_index("dp")
    across = ctx // CTX_ROWS
    interleaved = (
        hidden_rows.reshape(rows, CTX_ROWS, across, dp, piece)
        .transpose(3, 0, 2, 1, 4)
        .reshape(dp, rows, width)
    )
    received = [lax.dynamic_index_in_dim(interleaved, me, 0, keepdims=False)]
    for shift in range(1, dp):
        outgoing = lax.dynamic_index_in_dim(interleaved, (me + shift) % dp, 0, keepdims=False)
        pairs = [(i, (i + shift) % dp) for i in range(dp)]
        received.append(lax.ppermute(outgoing, "dp", pairs))
    return me, received


def weight_gradient(me, received, grad_all, grad_query_heads):
    partial = stacked_weight_product(me, received, grad_all)
    ctx = lax.axis_size("ctx")
    across = ctx // CTX_ROWS
    along_x = [[y * across + x for x in range(across)] for y in range(CTX_ROWS)]
    along_y = [[y * across + x for y in range(CTX_ROWS)] for x in range(across)]
    reduced = lax.psum_scatter(partial, "ctx", scatter_dimension=0, axis_index_groups=along_x, tiled=True)
    reduced, grad_query_heads = lax.optimization_barrier((reduced, grad_query_heads))
    grad_query = lax.all_to_all(grad_query_heads, "ctx", split_axis=0, concat_axis=1, tiled=True)
    reduced = lax.psum_scatter(reduced, "ctx", scatter_dimension=0, axis_index_groups=along_y, tiled=True)
    weight = lax.all_to_all(reduced.astype(jnp.float32), "dp", split_axis=1, concat_axis=0, tiled=True)
    return weight, grad_query


def local_body(queries, kv_proj, hidden, grad_out, doc_lengths, slab_offsets):
    query_matrix_rows = queries[0]
    upstream_gradient = grad_out[0]
    key_matrix_rows = kv_proj[0]
    hidden_rows = hidden[0]
    bounds = jnp.cumsum(doc_lengths[0], dtype=jnp.int32)
    offset = slab_offsets[0]
    key_value_width = 2 * KEY_VALUE_HEADS * HEAD_FEATURES
    repeat_heads = lax.axis_size("ctx") // KEY_VALUE_HEADS
    key_total_count = key_matrix_rows.shape[0]
    copies = jnp.broadcast_to(
        key_matrix_rows.reshape(key_total_count, KEY_VALUE_HEADS, 1, 2 * HEAD_FEATURES),
        (key_total_count, KEY_VALUE_HEADS, repeat_heads, 2 * HEAD_FEATURES),
    ).reshape(key_total_count, KEY_VALUE_HEADS * repeat_heads * 2 * HEAD_FEATURES)
    ctx = lax.axis_size("ctx")
    local_rows, query_width = query_matrix_rows.shape
    share = query_width // ctx
    pair = key_total_count // local_rows
    slot = 2 * HEAD_FEATURES
    merged = jnp.concatenate(
        [
            query_matrix_rows.reshape(local_rows, ctx, share),
            upstream_gradient.reshape(local_rows, ctx, share),
            copies.reshape(local_rows, pair, ctx, slot).transpose(0, 2, 1, 3).reshape(local_rows, ctx, pair * slot),
        ],
        axis=2,
    )
    arrived = lax.all_to_all(
        merged.reshape(local_rows, -1), "ctx", split_axis=1, concat_axis=0, tiled=True
    ).reshape(ctx, local_rows, -1)
    head_queries = arrived[:, :, :share].reshape(ctx * local_rows, share)
    head_upstream = arrived[:, :, share : 2 * share].reshape(ctx * local_rows, share)
    head_keys = arrived[:, :, 2 * share :].reshape(ctx * key_total_count, slot)
    me, received = send_hidden(hidden_rows)
    rows = head_queries.shape[0]
    keys = head_keys.shape[0]
    query_pos = offset + jnp.arange(rows, dtype=jnp.int32)
    key_pos = offset - WINDOW + jnp.arange(keys, dtype=jnp.int32)
    q_doc = doc_index(query_pos, bounds)
    k_doc = jnp.where(key_pos >= 0, doc_index(key_pos, bounds), -1)
    attended_heads, grad_query_heads, grad_head = head_attention(head_queries, head_upstream, head_keys, q_doc, k_doc)
    attended = lax.all_to_all(attended_heads, "ctx", split_axis=0, concat_axis=1, tiled=True)
    partial_sums = lax.all_to_all(
        grad_head.T.astype(jnp.bfloat16), "ctx", split_axis=0, concat_axis=1, tiled=True
    )
    grad_keys = jnp.sum(
        partial_sums.reshape(
            partial_sums.shape[0], KEY_VALUE_HEADS, repeat_heads, 2 * HEAD_FEATURES
        ).astype(jnp.float32),
        axis=2,
    ).reshape(partial_sums.shape[0], key_value_width)
    grad_low = grad_keys.astype(jnp.bfloat16)
    grad_all = lax.all_gather(grad_low, "dp", axis=0, tiled=False)
    attended, grad_all = lax.optimization_barrier((attended, grad_all))
    grad_weight, grad_query = weight_gradient(me, received, grad_all, grad_query_heads)
    return (attended[None], grad_query[None], grad_low[None], grad_weight)


def solution(mesh):
    in_specs = (
        P("dp", "ctx", None),
        P("dp", "ctx", None),
        P("dp", "ctx", None),
        P("dp", "ctx", None),
        P("dp", None),
        P("dp"),
    )
    out_specs = (P("dp", "ctx", None), P("dp", "ctx", None), P("dp", "ctx", None), P("ctx", "dp"))
    return jax.shard_map(local_body, mesh=mesh, in_specs=in_specs, out_specs=out_specs, check_vma=False)
```

```python
import functools

import jax
import jax.numpy as jnp
from jax import lax
from jax.experimental import pallas as pl
from jax.experimental.pallas import tpu as pltpu
from jax.sharding import PartitionSpec as P


HEAD_FEATURES = 128
KEY_VALUE_HEADS = 4
WINDOW = 2048
BLOCK_QUERIES = 256
CTX_ROWS = 4


def doc_index(positions, bounds):
    return jnp.sum(
        (bounds[None, :] <= positions[:, None]).astype(jnp.int32), axis=1, dtype=jnp.int32
    )


def attention_kernel(qdoc_ref, kdoc_ref, q_ref, go_ref, kv_ref, att_ref, dq_ref, dkv_ref, *, bq, span, heads):
    qb = pl.program_id(0)
    f32 = jnp.float32
    bf16 = jnp.bfloat16
    factor = HEAD_FEATURES ** (-0.5)

    @pl.when(qb == 0)
    def _():
        dkv_ref[...] = jnp.zeros_like(dkv_ref)

    start = pl.multiple_of(qb * bq, bq)
    k = kv_ref[pl.ds(start, span), 0:HEAD_FEATURES]
    v = kv_ref[pl.ds(start, span), HEAD_FEATURES : 2 * HEAD_FEATURES]
    nt = (((1,), (1,)), ((), ()))
    tn = (((0,), (0,)), ((), ()))
    row = lax.broadcasted_iota(jnp.int32, (bq, span), 0)
    col = lax.broadcasted_iota(jnp.int32, (bq, span), 1)
    same_doc = qdoc_ref[...] == kdoc_ref[:, pl.ds(start, span)]
    allowed = (col > row) & (col <= row + WINDOW) & same_doc
    for h in range(heads):
        cols = slice(h * HEAD_FEATURES, (h + 1) * HEAD_FEATURES)
        q = q_ref[:, cols]
        go = go_ref[:, cols]
        scores = lax.dot_general(q, k, nt, preferred_element_type=f32) * factor
        scores = jnp.where(allowed, scores, -1e30)
        maxima = jnp.max(scores, axis=1, keepdims=True)
        raised = jnp.exp(scores - maxima)
        weights = raised * (1.0 / jnp.sum(raised, axis=1, keepdims=True))
        weights_low = weights.astype(bf16)
        att = jnp.dot(weights_low, v, preferred_element_type=f32).astype(bf16)
        att_ref[:, cols] = att
        grad_probs = lax.dot_general(go, v, nt, preferred_element_type=f32)
        deltas = jnp.sum(go.astype(f32) * att.astype(f32), axis=1, keepdims=True)
        grad_scores = (weights * (grad_probs - deltas) * factor).astype(bf16)
        dq_ref[:, cols] = jnp.dot(grad_scores, k, preferred_element_type=f32).astype(bf16)
        dk = lax.dot_general(q, grad_scores, tn, preferred_element_type=f32)
        dv = lax.dot_general(go, weights_low, tn, preferred_element_type=f32)
        dkv_ref[0:HEAD_FEATURES, pl.ds(start, span)] += dk
        dkv_ref[HEAD_FEATURES : 2 * HEAD_FEATURES, pl.ds(start, span)] += dv


def head_attention(head_queries, head_upstream, head_keys, q_doc, k_doc):
    rows = head_queries.shape[0]
    keys = head_keys.shape[0]
    heads_here = head_queries.shape[1] // HEAD_FEATURES
    bq = min(BLOCK_QUERIES, rows)
    span = bq + WINDOW
    grid = (rows // bq,)
    kernel = functools.partial(attention_kernel, bq=bq, span=span, heads=heads_here)
    width = heads_here * HEAD_FEATURES
    flops = 12 * heads_here * rows * span * HEAD_FEATURES
    bytes_accessed = 2 * (4 * rows * heads_here * HEAD_FEATURES + keys * 2 * HEAD_FEATURES) + 4 * keys * 2 * HEAD_FEATURES
    return pl.pallas_call(
        kernel,
        grid=grid,
        in_specs=[
            pl.BlockSpec((bq, 1), lambda i: (i, 0)),
            pl.BlockSpec((1, keys), lambda i: (0, 0)),
            pl.BlockSpec((bq, width), lambda i: (i, 0)),
            pl.BlockSpec((bq, width), lambda i: (i, 0)),
            pl.BlockSpec((keys, 2 * HEAD_FEATURES), lambda i: (0, 0)),
        ],
        out_specs=[
            pl.BlockSpec((bq, width), lambda i: (i, 0)),
            pl.BlockSpec((bq, width), lambda i: (i, 0)),
            pl.BlockSpec((2 * HEAD_FEATURES, keys), lambda i: (0, 0)),
        ],
        out_shape=[
            jax.ShapeDtypeStruct(head_queries.shape, jnp.bfloat16),
            jax.ShapeDtypeStruct(head_queries.shape, jnp.bfloat16),
            jax.ShapeDtypeStruct((2 * HEAD_FEATURES, keys), jnp.float32),
        ],
        compiler_params=pltpu.CompilerParams(
            dimension_semantics=("arbitrary",),
            vmem_limit_bytes=60 * 1024 * 1024,
        ),
        cost_estimate=pl.CostEstimate(
            flops=flops, transcendentals=heads_here * rows * span, bytes_accessed=bytes_accessed
        ),
        name="band_attention",
    )(q_doc.reshape(rows, 1), k_doc.reshape(1, keys), head_queries, head_upstream, head_keys)


def weight_kernel(me_ref, *refs, parts):
    pieces, grad_ref, out_ref = refs[:parts], refs[parts], refs[parts + 1]
    me = me_ref[0]
    total = None
    for shift in range(parts):
        source = lax.rem(me - shift + parts, parts)
        term = lax.dot_general(
            pieces[shift][...], grad_ref[source], (((0,), (0,)), ((), ())),
            preferred_element_type=jnp.float32,
        )
        total = term if total is None else total + term
    out_ref[...] = total.astype(out_ref.dtype)


def stacked_weight_product(me, pieces, grad_all):
    parts = len(pieces)
    rows, width = pieces[0].shape
    columns = grad_all.shape[2]
    tile = 512 if width % 512 == 0 else width
    grid_spec = pltpu.PrefetchScalarGridSpec(
        num_scalar_prefetch=1,
        grid=(width // tile,),
        in_specs=[pl.BlockSpec((rows, tile), lambda i, me: (0, i)) for _ in range(parts)]
        + [pl.BlockSpec((parts, rows, columns), lambda i, me: (0, 0, 0))],
        out_specs=pl.BlockSpec((tile, columns), lambda i, me: (i, 0)),
    )
    return pl.pallas_call(
        functools.partial(weight_kernel, parts=parts),
        grid_spec=grid_spec,
        out_shape=jax.ShapeDtypeStruct((width, columns), jnp.bfloat16),
        compiler_params=pltpu.CompilerParams(
            dimension_semantics=("arbitrary",), vmem_limit_bytes=48 * 1024 * 1024
        ),
        cost_estimate=pl.CostEstimate(
            flops=2 * parts * rows * width * columns,
            transcendentals=0,
            bytes_accessed=2 * parts * rows * (width + columns) + 2 * width * columns,
        ),
        name="weight_product",
    )(jnp.reshape(me, (1,)).astype(jnp.int32), *pieces, grad_all)


def send_hidden(hidden_rows):
    dp = lax.axis_size("dp")
    ctx = lax.axis_size("ctx")
    rows, features = hidden_rows.shape
    piece = features // (ctx * dp)
    width = features // dp
    me = lax.axis_index("dp")
    across = ctx // CTX_ROWS
    interleaved = (
        hidden_rows.reshape(rows, CTX_ROWS, across, dp, piece)
        .transpose(3, 0, 2, 1, 4)
        .reshape(dp, rows, width)
    )
    received = [lax.dynamic_index_in_dim(interleaved, me, 0, keepdims=False)]
    for shift in range(1, dp):
        outgoing = lax.dynamic_index_in_dim(interleaved, (me + shift) % dp, 0, keepdims=False)
        pairs = [(i, (i + shift) % dp) for i in range(dp)]
        received.append(lax.ppermute(outgoing, "dp", pairs))
    return me, received


def weight_gradient(me, received, grad_all, grad_query_heads):
    partial = stacked_weight_product(me, received, grad_all)
    ctx = lax.axis_size("ctx")
    across = ctx // CTX_ROWS
    along_x = [[y * across + x for x in range(across)] for y in range(CTX_ROWS)]
    along_y = [[y * across + x for y in range(CTX_ROWS)] for x in range(across)]
    reduced = lax.psum_scatter(partial, "ctx", scatter_dimension=0, axis_index_groups=along_x, tiled=True)
    reduced, grad_query_heads = lax.optimization_barrier((reduced, grad_query_heads))
    grad_query = lax.all_to_all(grad_query_heads, "ctx", split_axis=0, concat_axis=1, tiled=True)
    reduced = lax.psum_scatter(reduced, "ctx", scatter_dimension=0, axis_index_groups=along_y, tiled=True)
    weight = lax.all_to_all(reduced.astype(jnp.float32), "dp", split_axis=1, concat_axis=0, tiled=True)
    return weight, grad_query


def local_body(queries, kv_proj, hidden, grad_out, doc_lengths, slab_offsets):
    query_matrix_rows = queries[0]
    upstream_gradient = grad_out[0]
    key_matrix_rows = kv_proj[0]
    hidden_rows = hidden[0]
    bounds = jnp.cumsum(doc_lengths[0], dtype=jnp.int32)
    offset = slab_offsets[0]
    key_value_width = 2 * KEY_VALUE_HEADS * HEAD_FEATURES
    repeat_heads = lax.axis_size("ctx") // KEY_VALUE_HEADS
    key_total_count = key_matrix_rows.shape[0]
    copies = jnp.broadcast_to(
        key_matrix_rows.reshape(key_total_count, KEY_VALUE_HEADS, 1, 2 * HEAD_FEATURES),
        (key_total_count, KEY_VALUE_HEADS, repeat_heads, 2 * HEAD_FEATURES),
    ).reshape(key_total_count, KEY_VALUE_HEADS * repeat_heads * 2 * HEAD_FEATURES)
    head_queries, head_upstream, head_keys = (
        lax.all_to_all(query_matrix_rows, "ctx", split_axis=1, concat_axis=0, tiled=True),
        lax.all_to_all(upstream_gradient, "ctx", split_axis=1, concat_axis=0, tiled=True),
        lax.all_to_all(copies, "ctx", split_axis=1, concat_axis=0, tiled=True),
    )
    me, received = send_hidden(hidden_rows)
    rows = head_queries.shape[0]
    keys = head_keys.shape[0]
    query_pos = offset + jnp.arange(rows, dtype=jnp.int32)
    key_pos = offset - WINDOW + jnp.arange(keys, dtype=jnp.int32)
    q_doc = doc_index(query_pos, bounds)
    k_doc = jnp.where(key_pos >= 0, doc_index(key_pos, bounds), -1)
    attended_heads, grad_query_heads, grad_head = head_attention(head_queries, head_upstream, head_keys, q_doc, k_doc)
    attended = lax.all_to_all(attended_heads, "ctx", split_axis=0, concat_axis=1, tiled=True)
    partial_sums = lax.all_to_all(
        grad_head.T.astype(jnp.bfloat16), "ctx", split_axis=0, concat_axis=1, tiled=True
    )
    grad_keys = jnp.sum(
        partial_sums.reshape(
            partial_sums.shape[0], KEY_VALUE_HEADS, repeat_heads, 2 * HEAD_FEATURES
        ).astype(jnp.float32),
        axis=2,
    ).reshape(partial_sums.shape[0], key_value_width)
    grad_low = grad_keys.astype(jnp.bfloat16)
    grad_all = lax.all_gather(grad_low, "dp", axis=0, tiled=False)
    attended, grad_all = lax.optimization_barrier((attended, grad_all))
    grad_weight, grad_query = weight_gradient(me, received, grad_all, grad_query_heads)
    return (attended[None], grad_query[None], grad_low[None], grad_weight)


def solution(mesh):
    in_specs = (
        P("dp", "ctx", None),
        P("dp", "ctx", None),
        P("dp", "ctx", None),
        P("dp", "ctx", None),
        P("dp", None),
        P("dp"),
    )
    out_specs = (P("dp", "ctx", None), P("dp", "ctx", None), P("dp", "ctx", None), P("ctx", "dp"))
    return jax.shard_map(local_body, mesh=mesh, in_specs=in_specs, out_specs=out_specs, check_vma=False)
```

```python
import functools

import jax
import jax.numpy as jnp
from jax import lax
from jax.experimental import pallas as pl
from jax.experimental.pallas import tpu as pltpu
from jax.sharding import PartitionSpec as P


HEAD_FEATURES = 128
KEY_VALUE_HEADS = 4
WINDOW = 2048
BLOCK_QUERIES = 512
CTX_ROWS = 4


def doc_index(positions, bounds):
    return jnp.sum(
        (bounds[None, :] <= positions[:, None]).astype(jnp.int32), axis=1, dtype=jnp.int32
    )


def attention_kernel(qdoc_ref, kdoc_ref, q_ref, go_ref, kv_ref, att_ref, dq_ref, dkv_ref, *, bq, span, heads):
    qb = pl.program_id(0)
    f32 = jnp.float32
    bf16 = jnp.bfloat16
    factor = HEAD_FEATURES ** (-0.5)

    @pl.when(qb == 0)
    def _():
        dkv_ref[...] = jnp.zeros_like(dkv_ref)

    start = pl.multiple_of(qb * bq, bq)
    k = kv_ref[pl.ds(start, span), 0:HEAD_FEATURES]
    v = kv_ref[pl.ds(start, span), HEAD_FEATURES : 2 * HEAD_FEATURES]
    nt = (((1,), (1,)), ((), ()))
    tn = (((0,), (0,)), ((), ()))
    row = lax.broadcasted_iota(jnp.int32, (bq, span), 0)
    col = lax.broadcasted_iota(jnp.int32, (bq, span), 1)
    same_doc = qdoc_ref[...] == kdoc_ref[:, pl.ds(start, span)]
    allowed = (col > row) & (col <= row + WINDOW) & same_doc
    for h in range(heads):
        cols = slice(h * HEAD_FEATURES, (h + 1) * HEAD_FEATURES)
        q = q_ref[:, cols]
        go = go_ref[:, cols]
        scores = lax.dot_general(q, k, nt, preferred_element_type=f32) * factor
        scores = jnp.where(allowed, scores, -1e30)
        maxima = jnp.max(scores, axis=1, keepdims=True)
        raised = jnp.exp(scores - maxima)
        weights = raised * (1.0 / jnp.sum(raised, axis=1, keepdims=True))
        weights_low = weights.astype(bf16)
        att = jnp.dot(weights_low, v, preferred_element_type=f32).astype(bf16)
        att_ref[:, cols] = att
        grad_probs = lax.dot_general(go, v, nt, preferred_element_type=f32)
        deltas = jnp.sum(go.astype(f32) * att.astype(f32), axis=1, keepdims=True)
        grad_scores = (weights * (grad_probs - deltas) * factor).astype(bf16)
        dq_ref[:, cols] = jnp.dot(grad_scores, k, preferred_element_type=f32).astype(bf16)
        dk = lax.dot_general(q, grad_scores, tn, preferred_element_type=f32)
        dv = lax.dot_general(go, weights_low, tn, preferred_element_type=f32)
        dkv_ref[0:HEAD_FEATURES, pl.ds(start, span)] += dk
        dkv_ref[HEAD_FEATURES : 2 * HEAD_FEATURES, pl.ds(start, span)] += dv


def head_attention(head_queries, head_upstream, head_keys, q_doc, k_doc):
    rows = head_queries.shape[0]
    keys = head_keys.shape[0]
    heads_here = head_queries.shape[1] // HEAD_FEATURES
    bq = min(BLOCK_QUERIES, rows)
    span = bq + WINDOW
    grid = (rows // bq,)
    kernel = functools.partial(attention_kernel, bq=bq, span=span, heads=heads_here)
    width = heads_here * HEAD_FEATURES
    flops = 12 * heads_here * rows * span * HEAD_FEATURES
    bytes_accessed = 2 * (4 * rows * heads_here * HEAD_FEATURES + keys * 2 * HEAD_FEATURES) + 4 * keys * 2 * HEAD_FEATURES
    return pl.pallas_call(
        kernel,
        grid=grid,
        in_specs=[
            pl.BlockSpec((bq, 1), lambda i: (i, 0)),
            pl.BlockSpec((1, keys), lambda i: (0, 0)),
            pl.BlockSpec((bq, width), lambda i: (i, 0)),
            pl.BlockSpec((bq, width), lambda i: (i, 0)),
            pl.BlockSpec((keys, 2 * HEAD_FEATURES), lambda i: (0, 0)),
        ],
        out_specs=[
            pl.BlockSpec((bq, width), lambda i: (i, 0)),
            pl.BlockSpec((bq, width), lambda i: (i, 0)),
            pl.BlockSpec((2 * HEAD_FEATURES, keys), lambda i: (0, 0)),
        ],
        out_shape=[
            jax.ShapeDtypeStruct(head_queries.shape, jnp.bfloat16),
            jax.ShapeDtypeStruct(head_queries.shape, jnp.bfloat16),
            jax.ShapeDtypeStruct((2 * HEAD_FEATURES, keys), jnp.float32),
        ],
        compiler_params=pltpu.CompilerParams(
            dimension_semantics=("arbitrary",), vmem_limit_bytes=60 * 1024 * 1024
        ),
        cost_estimate=pl.CostEstimate(
            flops=flops, transcendentals=heads_here * rows * span, bytes_accessed=bytes_accessed
        ),
        name="band_attention",
    )(q_doc.reshape(rows, 1), k_doc.reshape(1, keys), head_queries, head_upstream, head_keys)


def weight_kernel(me_ref, *refs, parts):
    pieces, grad_ref, out_ref = refs[:parts], refs[parts], refs[parts + 1]
    me = me_ref[0]
    total = None
    for shift in range(parts):
        source = lax.rem(me - shift + parts, parts)
        term = lax.dot_general(
            pieces[shift][...], grad_ref[source], (((0,), (0,)), ((), ())),
            preferred_element_type=jnp.float32,
        )
        total = term if total is None else total + term
    out_ref[...] = total.astype(out_ref.dtype)


def stacked_weight_product(me, pieces, grad_all):
    parts = len(pieces)
    rows, width = pieces[0].shape
    columns = grad_all.shape[2]
    tile = 512 if width % 512 == 0 else width
    grid_spec = pltpu.PrefetchScalarGridSpec(
        num_scalar_prefetch=1,
        grid=(width // tile,),
        in_specs=[pl.BlockSpec((rows, tile), lambda i, me: (0, i)) for _ in range(parts)]
        + [pl.BlockSpec((parts, rows, columns), lambda i, me: (0, 0, 0))],
        out_specs=pl.BlockSpec((tile, columns), lambda i, me: (i, 0)),
    )
    return pl.pallas_call(
        functools.partial(weight_kernel, parts=parts),
        grid_spec=grid_spec,
        out_shape=jax.ShapeDtypeStruct((width, columns), jnp.bfloat16),
        compiler_params=pltpu.CompilerParams(
            dimension_semantics=("arbitrary",), vmem_limit_bytes=48 * 1024 * 1024
        ),
        cost_estimate=pl.CostEstimate(
            flops=2 * parts * rows * width * columns,
            transcendentals=0,
            bytes_accessed=2 * parts * rows * (width + columns) + 2 * width * columns,
        ),
        name="weight_product",
    )(jnp.reshape(me, (1,)).astype(jnp.int32), *pieces, grad_all)


def send_hidden(hidden_rows):
    dp = lax.axis_size("dp")
    ctx = lax.axis_size("ctx")
    rows, features = hidden_rows.shape
    piece = features // (ctx * dp)
    width = features // dp
    me = lax.axis_index("dp")
    across = ctx // CTX_ROWS
    interleaved = (
        hidden_rows.reshape(rows, CTX_ROWS, across, dp, piece)
        .transpose(3, 0, 2, 1, 4)
        .reshape(dp, rows, width)
    )
    received = [lax.dynamic_index_in_dim(interleaved, me, 0, keepdims=False)]
    for shift in range(1, dp):
        outgoing = lax.dynamic_index_in_dim(interleaved, (me + shift) % dp, 0, keepdims=False)
        pairs = [(i, (i + shift) % dp) for i in range(dp)]
        received.append(lax.ppermute(outgoing, "dp", pairs))
    return me, received


def weight_gradient(me, received, grad_all, grad_query_heads):
    partial = stacked_weight_product(me, received, grad_all)
    ctx = lax.axis_size("ctx")
    across = ctx // CTX_ROWS
    along_x = [[y * across + x for x in range(across)] for y in range(CTX_ROWS)]
    along_y = [[y * across + x for y in range(CTX_ROWS)] for x in range(across)]
    reduced = lax.psum_scatter(partial, "ctx", scatter_dimension=0, axis_index_groups=along_x, tiled=True)
    reduced, grad_query_heads = lax.optimization_barrier((reduced, grad_query_heads))
    grad_query = lax.all_to_all(grad_query_heads, "ctx", split_axis=0, concat_axis=1, tiled=True)
    reduced = lax.psum_scatter(reduced, "ctx", scatter_dimension=0, axis_index_groups=along_y, tiled=True)
    weight = lax.all_to_all(reduced.astype(jnp.float32), "dp", split_axis=1, concat_axis=0, tiled=True)
    return weight, grad_query


def local_body(queries, kv_proj, hidden, grad_out, doc_lengths, slab_offsets):
    query_matrix_rows = queries[0]
    upstream_gradient = grad_out[0]
    key_matrix_rows = kv_proj[0]
    hidden_rows = hidden[0]
    bounds = jnp.cumsum(doc_lengths[0], dtype=jnp.int32)
    offset = slab_offsets[0]
    key_value_width = 2 * KEY_VALUE_HEADS * HEAD_FEATURES
    repeat_heads = lax.axis_size("ctx") // KEY_VALUE_HEADS
    key_total_count = key_matrix_rows.shape[0]
    copies = jnp.broadcast_to(
        key_matrix_rows.reshape(key_total_count, KEY_VALUE_HEADS, 1, 2 * HEAD_FEATURES),
        (key_total_count, KEY_VALUE_HEADS, repeat_heads, 2 * HEAD_FEATURES),
    ).reshape(key_total_count, KEY_VALUE_HEADS * repeat_heads * 2 * HEAD_FEATURES)
    head_queries, head_upstream, head_keys = (
        lax.all_to_all(query_matrix_rows, "ctx", split_axis=1, concat_axis=0, tiled=True),
        lax.all_to_all(upstream_gradient, "ctx", split_axis=1, concat_axis=0, tiled=True),
        lax.all_to_all(copies, "ctx", split_axis=1, concat_axis=0, tiled=True),
    )
    me, received = send_hidden(hidden_rows)
    rows = head_queries.shape[0]
    keys = head_keys.shape[0]
    query_pos = offset + jnp.arange(rows, dtype=jnp.int32)
    key_pos = offset - WINDOW + jnp.arange(keys, dtype=jnp.int32)
    q_doc = doc_index(query_pos, bounds)
    k_doc = jnp.where(key_pos >= 0, doc_index(key_pos, bounds), -1)
    attended_heads, grad_query_heads, grad_head = head_attention(head_queries, head_upstream, head_keys, q_doc, k_doc)
    attended = lax.all_to_all(attended_heads, "ctx", split_axis=0, concat_axis=1, tiled=True)
    partial_sums = lax.all_to_all(
        grad_head.T.astype(jnp.bfloat16), "ctx", split_axis=0, concat_axis=1, tiled=True
    )
    grad_keys = jnp.sum(
        partial_sums.reshape(
            partial_sums.shape[0], KEY_VALUE_HEADS, repeat_heads, 2 * HEAD_FEATURES
        ).astype(jnp.float32),
        axis=2,
    ).reshape(partial_sums.shape[0], key_value_width)
    grad_low = grad_keys.astype(jnp.bfloat16)
    grad_all = lax.all_gather(grad_low, "dp", axis=0, tiled=False)
    attended, grad_all = lax.optimization_barrier((attended, grad_all))
    grad_weight, grad_query = weight_gradient(me, received, grad_all, grad_query_heads)
    return (attended[None], grad_query[None], grad_low[None], grad_weight)


def solution(mesh):
    in_specs = (
        P("dp", "ctx", None),
        P("dp", "ctx", None),
        P("dp", "ctx", None),
        P("dp", "ctx", None),
        P("dp", None),
        P("dp"),
    )
    out_specs = (P("dp", "ctx", None), P("dp", "ctx", None), P("dp", "ctx", None), P("ctx", "dp"))
    return jax.shard_map(local_body, mesh=mesh, in_specs=in_specs, out_specs=out_specs, check_vma=False)
```
